256 devices in a mesh: pipe: 16 (over z, x_lo), ctx: 16 (over x_hi, y, core).
Axes of the slice: x: 4 (x_hi: 2, x_lo: 2; x = x_hi * 2 + x_lo), y: 4, z: 8, core: 2. Of those that a mesh axis runs over, the one named last changes fastest.
Arguments:
- forward_in: bfloat16 [16, 2, 512, 8192], P('pipe', None, 'ctx'), may hold values from -8 to 8
- backward_in: bfloat16 [16, 2, 512, 8192], P('pipe', None, 'ctx'), may hold values from -8 to 8
- grad_out: bfloat16 [16, 2, 512, 8192], P('pipe', None, 'ctx'), may hold values from -6 to 6
- cached_keys: bfloat16 [16, 2, 512, 8, 128], P('pipe', None, 'ctx'), may hold values from -21 to 21
- cached_values: bfloat16 [16, 2, 512, 8, 128], P('pipe', None, 'ctx'), may hold values from -6 to 6
- norm_gain: float32 [16, 2, 8192], P('pipe'), may hold values from 0.25 to 1.75
- key_weight: bfloat16 [16, 2, 8192, 1024], P('pipe', None, 'ctx'), may hold values from -0.0625 to 0.0625
- value_weight: bfloat16 [16, 2, 8192, 1024], P('pipe', None, 'ctx'), may hold values from -0.0625 to 0.0625
- segment_index: int32 [16, 2, 2], P('pipe'), may hold values from 0 to 1, as said below
Outputs:
- next_forward: bfloat16 [16, 2, 512, 8192], P('pipe', None, 'ctx')
- next_backward: bfloat16 [16, 2, 512, 8192], P('pipe', None, 'ctx')
The draws below stay inside these ranges and needn't reach their ends.
Inputs may be any that keep to these rules, and one draw needn't show every extreme that they name: `segment_index`: the largest segment index, 1, occurs in every draw.
All inputs are finite; a program needn't handle non-finite values.
Results may differ from the reference program's by a relative error of at most 0.04.
Values may be sent and summed in bfloat16 or wider, within the bound.
No kernel may reach another device: no remote copies, remote signals or barrier semaphores. Data moves between devices by JAX's collectives and lax.ppermute only.
A program may use at most 128 MiB of HBM per device.

```python
import jax
import jax.numpy as jnp
from jax import lax

D = 8192
H = 64
KVH = 8
HS = 128
SEG = 512
STRETCHES = 2
CACHE = 512
N_PIPE = 16
N_CTX = 16


def residual_rows(key, shape):
    first_key = jax.random.fold_in(key, 101)
    values = jnp.clip(jax.random.normal(first_key, shape, jnp.float32), -6.0, 6.0)
    return values.astype(jnp.bfloat16)


def draw_forward_in(key, part):
    return residual_rows(jax.random.fold_in(key, 1), (N_PIPE, STRETCHES, SEG, D))


def draw_backward_in(key, part):
    return residual_rows(jax.random.fold_in(key, 2), (N_PIPE, STRETCHES, SEG, D))


def draw_cached_keys(key, part):
    shape = (N_PIPE, STRETCHES, CACHE, KVH, HS)
    first_key = jax.random.fold_in(key, 201)
    values = jnp.clip(jax.random.normal(first_key, shape, jnp.float32), -6.0, 6.0)
    return values.astype(jnp.bfloat16)


def draw_segment_index(key, part):
    highest = CACHE // SEG
    count = N_PIPE * STRETCHES * 2
    drawn = jax.random.randint(jax.random.fold_in(key, 301), (count,), 0, highest + 1)
    spot = jax.random.randint(jax.random.fold_in(key, 302), (), 0, count)
    places = jnp.arange(count, dtype=jnp.int32)
    drawn = jnp.where(places == spot, highest, drawn)
    return drawn.reshape(N_PIPE, STRETCHES, 2).astype(jnp.int32)


def level_of(rng, extent, cuts, smallest, high):
    def one(dim, shards_of):
        heights = jax.random.uniform(jax.random.fold_in(jax.random.fold_in(rng, 6), dim), (shards_of,), jnp.float32, smallest / len(cuts), high / len(cuts))
        return jnp.repeat(jnp.exp(heights), extent[dim] // shards_of).reshape((-1,) + (1,) * (len(extent) - dim - 1))

    gain = one(*cuts[0])
    for cut in cuts[1:]:
        gain = gain * one(*cut)
    return gain


def scatter_about(key, dims, deviation, bound, shards=(), kind=jnp.bfloat16):
    values = deviation * jax.random.normal(key, dims, jnp.float32)
    if shards:
        values = values * level_of(key, dims, shards, -0.22, 0.18)
    return jnp.clip(values, -bound, bound).astype(kind)


def setup_inputs(seed: int = 0) -> dict:
    seeds = jax.random.split(jax.random.key(seed), 10)
    return {
        "forward_in": draw_forward_in(jax.random.fold_in(seeds[9], 71), 0),
        "backward_in": draw_backward_in(jax.random.fold_in(seeds[9], 71), 0),
        "grad_out": scatter_about(seeds[2], (N_PIPE, STRETCHES, SEG, D), 1.0, 6.0, ((0, 16), (2, 16))),
        "cached_keys": draw_cached_keys(jax.random.fold_in(seeds[9], 71), 0),
        "cached_values": scatter_about(seeds[4], (N_PIPE, STRETCHES, CACHE, KVH, HS), 1.0, 6.0, ((0, 16), (2, 16))),
        "norm_gain": jnp.clip(1.0 + 0.15 * jax.random.normal(seeds[5], (N_PIPE, STRETCHES, D), jnp.float32), 0.25, 1.75),
        "key_weight": scatter_about(seeds[6], (N_PIPE, STRETCHES, D, KVH * HS), D ** -0.5, 0.0625, ((0, 16), (2, 16))),
        "value_weight": scatter_about(seeds[7], (N_PIPE, STRETCHES, D, KVH * HS), D ** -0.5, 0.0625, ((0, 16), (2, 16))),
        "segment_index": draw_segment_index(jax.random.fold_in(seeds[9], 71), 0),
    }


NEGATIVE = -1e+30

def normalize(in_rows, gain_row):
    as_float = in_rows.astype(jnp.float32)
    inverse = lax.rsqrt(lax.optimization_barrier(jnp.mean(as_float * as_float, axis=-1, keepdims=True)) + 1e-05)
    normed = as_float * inverse
    return (normed, inverse, (normed * gain_row).astype(jnp.bfloat16))

def block_product(activations, weight):
    tokens = activations.shape[0]
    pieces = activations.reshape(tokens, N_CTX, D // N_CTX).astype(jnp.float32)
    weight_pieces = weight.reshape(N_CTX, D // N_CTX, KVH * HS).astype(jnp.float32)
    partial_value = jnp.einsum('tnf,nfe->nte', pieces, weight_pieces)
    rounded = lax.optimization_barrier(partial_value.astype(jnp.bfloat16)).astype(jnp.float32)
    return lax.optimization_barrier(jnp.sum(rounded, axis=0)).astype(jnp.bfloat16)

def project_kv(activations, key_weight, value_weight):
    tokens = activations.shape[0]
    new_keys = block_product(activations, key_weight)
    new_values = block_product(activations, value_weight)
    return (new_keys.reshape(tokens, KVH, HS), new_values.reshape(tokens, KVH, HS))

def probabilities(queries, key_list, position):
    factor = HS ** (-0.5)
    scores = jnp.einsum('tkgd,skd->kgts', queries.astype(jnp.float32), key_list.astype(jnp.float32)) * factor
    column = lax.broadcasted_iota(jnp.int32, (SEG, key_list.shape[0]), 1)
    row_ids = lax.broadcasted_iota(jnp.int32, (SEG, key_list.shape[0]), 0)
    visible = jnp.where(column < CACHE, column < position * SEG, column - CACHE <= row_ids)
    scores = jnp.where(visible, scores, NEGATIVE)
    row_max = lax.optimization_barrier(jnp.max(scores, axis=-1, keepdims=True))
    lifted = jnp.exp(scores - row_max)
    return lifted / lax.optimization_barrier(jnp.sum(lifted, axis=-1, keepdims=True))

def attend(queries, key_list, value_list, position):
    prob_full = probabilities(queries, key_list, position)
    prob_half = prob_full.astype(jnp.bfloat16)
    attended = jnp.einsum('kgts,skd->tkgd', prob_half.astype(jnp.float32), value_list.astype(jnp.float32))
    return (prob_full, prob_half, attended.astype(jnp.bfloat16))

def run_total(per_head):
    run_len = min(H // N_CTX, H // KVH)
    tokens = per_head.shape[0]
    runs = per_head.reshape(tokens, KVH, H // KVH // run_len, run_len, HS)
    partial_sums = lax.optimization_barrier(lax.optimization_barrier(jnp.sum(runs, axis=3)).astype(jnp.bfloat16)).astype(jnp.float32)
    return lax.optimization_barrier(jnp.sum(partial_sums, axis=2)).astype(jnp.bfloat16)

def attend_back(queries, key_list, value_list, position, grad_heads):
    prob_full, prob_half, attended = attend(queries, key_list, value_list, position)
    grad_wide = grad_heads.astype(jnp.float32)
    grad_prob = jnp.einsum('tkgd,skd->kgts', grad_wide, value_list.astype(jnp.float32))
    row_delta = lax.optimization_barrier(jnp.sum(grad_wide * attended.astype(jnp.float32), axis=-1))
    row_delta = jnp.transpose(row_delta, (1, 2, 0))[..., None]
    grad_score = (prob_full * (grad_prob - row_delta) * HS ** (-0.5)).astype(jnp.bfloat16)
    grad_query = jnp.einsum('kgts,skd->tkgd', grad_score.astype(jnp.float32), key_list.astype(jnp.float32)).astype(jnp.bfloat16)
    own_score = grad_score[..., CACHE:].astype(jnp.float32)
    own_weight = prob_half[..., CACHE:].astype(jnp.float32)
    key_heads = jnp.einsum('kgts,tkgd->skgd', own_score, queries.astype(jnp.float32))
    value_heads = jnp.einsum('kgts,tkgd->skgd', own_weight, grad_wide)
    return (grad_query, run_total(key_heads), run_total(value_heads))

def input_grad(in_rows, gain_row, key_weight, value_weight, grad_query, grad_key, grad_value, grad_rows):
    parts = normalize(in_rows, gain_row)
    normed = parts[0]
    inverse = parts[1]
    tokens = in_rows.shape[0]
    back_rows = jnp.dot(grad_key.reshape(tokens, KVH * HS), key_weight.T, preferred_element_type=jnp.float32)
    back_rows = back_rows + jnp.dot(grad_value.reshape(tokens, KVH * HS), value_weight.T, preferred_element_type=jnp.float32)
    grad_acts = (grad_query.astype(jnp.float32).reshape(tokens, D) + back_rows).astype(jnp.bfloat16)
    grad_normed = grad_acts.astype(jnp.float32) * gain_row
    grad_input = inverse * (grad_normed - normed * lax.optimization_barrier(jnp.mean(grad_normed * normed, axis=-1, keepdims=True)))
    return (grad_rows.astype(jnp.float32) + grad_input).astype(jnp.bfloat16)

def one_section(section_args):
    forward_rows, backward_rows, grad_rows, keys_cached, values_cached, gain_row, key_weight, value_weight, section_segments = section_args
    forward_acts = normalize(forward_rows, gain_row)[2]
    forward_keys, forward_values = project_kv(forward_acts, key_weight, value_weight)
    key_list = jnp.concatenate([keys_cached, forward_keys], axis=0)
    value_list = jnp.concatenate([values_cached, forward_values], axis=0)
    attended = attend(forward_acts.reshape(SEG, KVH, H // KVH, HS), key_list, value_list, section_segments[0])[2]
    section_out = (forward_rows.astype(jnp.float32) + attended.reshape(SEG, D).astype(jnp.float32)).astype(jnp.bfloat16)
    backward_acts = normalize(backward_rows, gain_row)[2]
    backward_keys, backward_values = project_kv(backward_acts, key_weight, value_weight)
    back_keys = jnp.concatenate([keys_cached, backward_keys], axis=0)
    back_values = jnp.concatenate([values_cached, backward_values], axis=0)
    grad_query, grad_key, grad_value = attend_back(backward_acts.reshape(SEG, KVH, H // KVH, HS), back_keys, back_values, section_segments[1], grad_rows.reshape(SEG, KVH, H // KVH, HS))
    section_grad = input_grad(backward_rows, gain_row, key_weight, value_weight, grad_query, grad_key, grad_value, grad_rows)
    return (section_out, section_grad)

def flatten(block):
    swapped = jnp.swapaxes(block, 0, 1)
    return swapped.reshape((STRETCHES * N_PIPE,) + block.shape[2:])

def unflatten(stacked):
    return jnp.swapaxes(stacked.reshape((STRETCHES, N_PIPE) + stacked.shape[1:]), 0, 1)

def reference(forward_in, backward_in, grad_out, cached_keys, cached_values, norm_gain, key_weight, value_weight, segment_index):
    stacked = tuple((flatten(member) for member in (forward_in, backward_in, grad_out, cached_keys, cached_values, norm_gain, key_weight, value_weight, segment_index)))
    outs_forward, outs_backward = lax.map(one_section, stacked)
    next_forward = unflatten(jnp.roll(outs_forward, 1, axis=0))
    next_backward = unflatten(jnp.roll(outs_backward, -1, axis=0))
    return (next_forward, next_backward)
```

```python
import jax
import jax.numpy as jnp
from jax import lax
from jax.sharding import PartitionSpec as P

NEGATIVE = -1e30


def passed_along(array, axis, by):
    count = lax.axis_size(axis)
    return lax.ppermute(array, axis, [(i, (i + by) % count) for i in range(count)])


def swapped_pairs(array, axis):
    count = lax.axis_size(axis)
    return lax.ppermute(array, axis, [(i, i ^ 1) for i in range(count)])


def normalize(in_rows, gain_row):
    as_float = in_rows.astype(jnp.float32)
    inverse = lax.rsqrt(jnp.mean(as_float * as_float, axis=-1, keepdims=True) + 1e-05)
    normed = as_float * inverse
    return (normed, inverse, (normed * gain_row).astype(jnp.bfloat16))


def probabilities(queries, key_list, position, cache_len):
    seg_len = queries.shape[0]
    factor = queries.shape[-1] ** (-0.5)
    scores = (
        jnp.einsum("tgd,sd->gts", queries, key_list, preferred_element_type=jnp.float32) * factor
    )
    column = lax.broadcasted_iota(jnp.int32, (seg_len, key_list.shape[0]), 1)
    row_ids = lax.broadcasted_iota(jnp.int32, (seg_len, key_list.shape[0]), 0)
    visible = jnp.where(
        column < cache_len, column < position * seg_len, column - cache_len <= row_ids
    )
    scores = jnp.where(visible, scores, NEGATIVE)
    row_max = jnp.max(scores, axis=-1, keepdims=True)
    lifted = jnp.exp(scores - row_max)
    return lifted / jnp.sum(lifted, axis=-1, keepdims=True)


def attend(queries, key_list, value_list, position, cache_len):
    prob_full = probabilities(queries, key_list, position, cache_len)
    prob_half = prob_full.astype(jnp.bfloat16)
    attended = jnp.einsum(
        "gts,sd->tgd", prob_half, value_list, preferred_element_type=jnp.float32
    )
    return (prob_full, prob_half, attended.astype(jnp.bfloat16))


def attend_back(queries, key_list, value_list, position, cache_len, grad_heads):
    prob_full, prob_half, attended = attend(queries, key_list, value_list, position, cache_len)
    grad_prob = jnp.einsum(
        "tgd,sd->gts", grad_heads, value_list, preferred_element_type=jnp.float32
    )
    row_delta = jnp.sum(grad_heads.astype(jnp.float32) * attended.astype(jnp.float32), axis=-1)
    row_delta = jnp.transpose(row_delta, (1, 0))[..., None]
    factor = queries.shape[-1] ** (-0.5)
    grad_score = (prob_full * (grad_prob - row_delta) * factor).astype(jnp.bfloat16)
    grad_query = jnp.einsum(
        "gts,sd->tgd", grad_score, key_list, preferred_element_type=jnp.float32
    ).astype(jnp.bfloat16)
    grad_key = jnp.einsum(
        "gts,tgd->sd", grad_score[..., cache_len:], queries, preferred_element_type=jnp.float32
    )
    grad_value = jnp.einsum(
        "gts,tgd->sd", prob_half[..., cache_len:], grad_heads, preferred_element_type=jnp.float32
    )
    return (grad_query, grad_key.astype(jnp.bfloat16), grad_value.astype(jnp.bfloat16))


def input_grad(in_rows, gain_row, grad_acts, grad_rows):
    parts = normalize(in_rows, gain_row)
    normed = parts[0]
    inverse = parts[1]
    grad_normed = grad_acts.astype(jnp.float32) * gain_row
    grad_input = inverse * (
        grad_normed - normed * jnp.mean(grad_normed * normed, axis=-1, keepdims=True)
    )
    return (grad_rows.astype(jnp.float32) + grad_input).astype(jnp.bfloat16)


def on_device(
    forward_in,
    backward_in,
    grad_out,
    cached_keys,
    cached_values,
    norm_gain,
    key_weight,
    value_weight,
    segment_index,
):
    ctx_size = lax.axis_size("ctx")
    rank_id = lax.axis_index("ctx")
    stretch_count = forward_in.shape[1]
    local_rows = forward_in.shape[2]
    model_width = forward_in.shape[3]
    kv_count = cached_keys.shape[3]
    head_size = cached_keys.shape[4]
    seg_len = local_rows * ctx_size
    cache_local = cached_keys.shape[2]
    cache_len = cache_local * ctx_size
    head_count = model_width // head_size
    group_size = head_count // kv_count
    local_heads = head_count // ctx_size
    local_width = model_width // ctx_size
    kv_width = kv_count * head_size
    piece = kv_width // ctx_size
    copies = ctx_size // kv_count
    is_even = rank_id % 2 == 0

    def per_owner(cache):
        picked = jnp.repeat(cache[0], copies, axis=2)
        return jnp.transpose(picked, (1, 2, 0, 3)).reshape(cache_local, ctx_size, -1)

    cache_rows = jnp.concatenate([per_owner(cached_keys), per_owner(cached_values)], axis=-1)

    forward_outs = []
    backward_outs = []
    for stretch in range(stretch_count):
        gain_row = norm_gain[0, stretch]
        key_rows = key_weight[0, stretch]
        value_rows = value_weight[0, stretch]
        forward_rows = forward_in[0, stretch]
        backward_rows = backward_in[0, stretch]
        grad_rows = grad_out[0, stretch]
        forward_acts = normalize(forward_rows, gain_row)[2]
        backward_acts = normalize(backward_rows, gain_row)[2]
        outgoing = [
            forward_acts.reshape(local_rows, ctx_size, local_width),
            backward_acts.reshape(local_rows, ctx_size, local_width),
            grad_rows.reshape(local_rows, ctx_size, local_width),
        ]
        if stretch == 0:
            outgoing.append(cache_rows)
        sent = lax.all_to_all(
            jnp.stack(outgoing), "ctx", split_axis=2, concat_axis=1, tiled=True
        )
        if stretch == 0:
            cache_heads = sent[3].reshape(cache_len, 2, stretch_count, head_size)
        forward_slice = sent[0].reshape(seg_len, local_width)
        backward_slice = sent[1].reshape(seg_len, local_width)
        grad_slice = sent[2].reshape(seg_len, local_width)
        both_slices = jnp.stack([forward_slice, backward_slice])
        key_pieces = key_rows.reshape(local_width, ctx_size, piece)
        value_pieces = value_rows.reshape(local_width, ctx_size, piece)
        partial_value = jnp.stack(
            [
                jnp.einsum("btf,fce->bcte", both_slices, key_pieces, preferred_element_type=jnp.float32),
                jnp.einsum("btf,fce->bcte", both_slices, value_pieces, preferred_element_type=jnp.float32),
            ],
            axis=1,
        ).astype(jnp.bfloat16)
        mine = lax.psum_scatter(
            partial_value.reshape(4, ctx_size, -1), "ctx", scatter_dimension=1, tiled=True
        ).reshape(2, 2, seg_len, piece)
        theirs = swapped_pairs(mine, "ctx")
        new_kv = jnp.where(
            is_even,
            jnp.concatenate([mine, theirs], axis=-1),
            jnp.concatenate([theirs, mine], axis=-1),
        )
        cached_k = cache_heads[:, 0, stretch]
        cached_v = cache_heads[:, 1, stretch]
        forward_key_list = jnp.concatenate([cached_k, new_kv[0, 0]], axis=0)
        forward_value_list = jnp.concatenate([cached_v, new_kv[0, 1]], axis=0)
        backward_key_list = jnp.concatenate([cached_k, new_kv[1, 0]], axis=0)
        backward_value_list = jnp.concatenate([cached_v, new_kv[1, 1]], axis=0)
        attended = attend(
            forward_slice.reshape(seg_len, local_heads, head_size),
            forward_key_list,
            forward_value_list,
            segment_index[0, stretch, 0],
            cache_len,
        )[2]
        grad_query, grad_key, grad_value = attend_back(
            backward_slice.reshape(seg_len, local_heads, head_size),
            backward_key_list,
            backward_value_list,
            segment_index[0, stretch, 1],
            cache_len,
            grad_slice.reshape(seg_len, local_heads, head_size),
        )
        run_sums = jnp.stack([grad_key, grad_value])
        other_run = swapped_pairs(run_sums, "ctx")
        head_grads = (run_sums.astype(jnp.float32) + other_run.astype(jnp.float32)).astype(
            jnp.bfloat16
        )
        half_rows = seg_len // 2
        my_half = lax.dynamic_slice_in_dim(head_grads, (rank_id % 2) * half_rows, half_rows, 1)
        every_half = lax.all_gather(my_half, "ctx", axis=0, tiled=False)
        every_half = every_half.reshape(kv_count, 2, 2, half_rows, head_size)
        key_rows_heads = key_rows.reshape(local_width, kv_count, head_size)
        value_rows_heads = value_rows.reshape(local_width, kv_count, head_size)
        back_rows = jnp.einsum(
            "jhtd,fjd->htf", every_half[:, :, 0], key_rows_heads, preferred_element_type=jnp.float32
        )
        back_rows = back_rows + jnp.einsum(
            "jhtd,fjd->htf",
            every_half[:, :, 1],
            value_rows_heads,
            preferred_element_type=jnp.float32,
        )
        grad_acts = (
            grad_query.reshape(seg_len, -1).astype(jnp.float32) + back_rows.reshape(seg_len, -1)
        ).astype(jnp.bfloat16)
        returned = lax.all_to_all(
            jnp.stack([attended.reshape(ctx_size, local_rows, -1), grad_acts.reshape(ctx_size, local_rows, -1)]),
            "ctx",
            split_axis=1,
            concat_axis=3,
            tiled=True,
        )
        attn_rows = returned[0].reshape(local_rows, model_width)
        section_out = (forward_rows.astype(jnp.float32) + attn_rows.astype(jnp.float32)).astype(
            jnp.bfloat16
        )
        section_grad = input_grad(
            backward_rows, gain_row, returned[1].reshape(local_rows, model_width), grad_rows
        )
        forward_outs.append(passed_along(section_out, "pipe", 1))
        backward_outs.append(passed_along(section_grad, "pipe", -1))
    pipe_rank = lax.axis_index("pipe")
    arrived = jnp.stack(forward_outs)
    next_forward = jnp.where(pipe_rank == 0, jnp.roll(arrived, 1, axis=0), arrived)
    came_back = jnp.stack(backward_outs)
    next_backward = jnp.where(
        pipe_rank == lax.axis_size("pipe") - 1, jnp.roll(came_back, -1, axis=0), came_back
    )
    return (next_forward[None], next_backward[None])


def solution(mesh):
    in_specs = (
        P("pipe", None, "ctx", None),
        P("pipe", None, "ctx", None),
        P("pipe", None, "ctx", None),
        P("pipe", None, "ctx", None, None),
        P("pipe", None, "ctx", None, None),
        P("pipe", None, None),
        P("pipe", None, "ctx", None),
        P("pipe", None, "ctx", None),
        P("pipe", None, None),
    )
    out_specs = (P("pipe", None, "ctx", None), P("pipe", None, "ctx", None))
    return jax.shard_map(
        on_device, mesh=mesh, in_specs=in_specs, out_specs=out_specs, check_vma=False
    )
```

```python
import jax
import jax.numpy as jnp
from jax import lax
from jax.sharding import PartitionSpec as P

NEGATIVE = -1e30


def passed_along(array, axis, by):
    count = lax.axis_size(axis)
    return lax.ppermute(array, axis, [(i, (i + by) % count) for i in range(count)])


def swapped_pairs(array, axis):
    count = lax.axis_size(axis)
    return lax.ppermute(array, axis, [(i, i ^ 1) for i in range(count)])


def swapped_with(array, axis, mask):
    count = lax.axis_size(axis)
    return lax.ppermute(array, axis, [(i, i ^ mask) for i in range(count)])


def reduce_to_head(partial, rank_id, ctx_size):
    rows = partial.shape[1]
    core = rank_id % 2
    half = rows // 2
    kept = lax.dynamic_slice_in_dim(partial, core * half, half, 1)
    given = lax.dynamic_slice_in_dim(partial, (1 - core) * half, half, 1)
    total = kept.astype(jnp.float32) + swapped_with(given, "ctx", 1).astype(jnp.float32)
    mask = ctx_size // 2
    while mask > 1:
        bit = (rank_id // mask) % 2
        width = total.shape[2] // 2
        kept = lax.dynamic_slice_in_dim(total, bit * width, width, 2)
        given = lax.dynamic_slice_in_dim(total, (1 - bit) * width, width, 2)
        total = kept + swapped_with(given.astype(jnp.bfloat16), "ctx", mask).astype(jnp.float32)
        mask //= 2
    mine = total.astype(jnp.bfloat16)
    theirs = swapped_with(mine, "ctx", 1)
    return jnp.where(
        core == 0,
        jnp.concatenate([mine, theirs], axis=1),
        jnp.concatenate([theirs, mine], axis=1),
    )


def normalize(in_rows, gain_row):
    as_float = in_rows.astype(jnp.float32)
    inverse = lax.rsqrt(jnp.mean(as_float * as_float, axis=-1, keepdims=True) + 1e-05)
    normed = as_float * inverse
    return (normed, inverse, (normed * gain_row).astype(jnp.bfloat16))


def probabilities(queries, key_list, position, cache_len):
    seg_len = queries.shape[0]
    factor = queries.shape[-1] ** (-0.5)
    scores = (
        jnp.einsum("tgd,sd->gts", queries, key_list, preferred_element_type=jnp.float32) * factor
    )
    column = lax.broadcasted_iota(jnp.int32, (seg_len, key_list.shape[0]), 1)
    row_ids = lax.broadcasted_iota(jnp.int32, (seg_len, key_list.shape[0]), 0)
    visible = jnp.where(
        column < cache_len, column < position * seg_len, column - cache_len <= row_ids
    )
    scores = jnp.where(visible, scores, NEGATIVE)
    row_max = jnp.max(scores, axis=-1, keepdims=True)
    lifted = jnp.exp(scores - row_max)
    return lifted / jnp.sum(lifted, axis=-1, keepdims=True)


def attend(queries, key_list, value_list, position, cache_len):
    prob_full = probabilities(queries, key_list, position, cache_len)
    prob_half = prob_full.astype(jnp.bfloat16)
    attended = jnp.einsum(
        "gts,sd->tgd", prob_half, value_list, preferred_element_type=jnp.float32
    )
    return (prob_full, prob_half, attended.astype(jnp.bfloat16))


def attend_back(queries, key_list, value_list, position, cache_len, grad_heads):
    prob_full, prob_half, attended = attend(queries, key_list, value_list, position, cache_len)
    grad_prob = jnp.einsum(
        "tgd,sd->gts", grad_heads, value_list, preferred_element_type=jnp.float32
    )
    row_delta = jnp.sum(grad_heads.astype(jnp.float32) * attended.astype(jnp.float32), axis=-1)
    row_delta = jnp.transpose(row_delta, (1, 0))[..., None]
    factor = queries.shape[-1] ** (-0.5)
    grad_score = (prob_full * (grad_prob - row_delta) * factor).astype(jnp.bfloat16)
    grad_query = jnp.einsum(
        "gts,sd->tgd", grad_score, key_list, preferred_element_type=jnp.float32
    ).astype(jnp.bfloat16)
    grad_key = jnp.einsum(
        "gts,tgd->sd", grad_score[..., cache_len:], queries, preferred_element_type=jnp.float32
    )
    grad_value = jnp.einsum(
        "gts,tgd->sd", prob_half[..., cache_len:], grad_heads, preferred_element_type=jnp.float32
    )
    return (grad_query, grad_key.astype(jnp.bfloat16), grad_value.astype(jnp.bfloat16))


def input_grad(in_rows, gain_row, grad_acts, grad_rows):
    parts = normalize(in_rows, gain_row)
    normed = parts[0]
    inverse = parts[1]
    grad_normed = grad_acts.astype(jnp.float32) * gain_row
    grad_input = inverse * (
        grad_normed - normed * jnp.mean(grad_normed * normed, axis=-1, keepdims=True)
    )
    return (grad_rows.astype(jnp.float32) + grad_input).astype(jnp.bfloat16)


def on_device(
    forward_in,
    backward_in,
    grad_out,
    cached_keys,
    cached_values,
    norm_gain,
    key_weight,
    value_weight,
    segment_index,
):
    ctx_size = lax.axis_size("ctx")
    rank_id = lax.axis_index("ctx")
    stretch_count = forward_in.shape[1]
    local_rows = forward_in.shape[2]
    model_width = forward_in.shape[3]
    kv_count = cached_keys.shape[3]
    head_size = cached_keys.shape[4]
    seg_len = local_rows * ctx_size
    cache_local = cached_keys.shape[2]
    cache_len = cache_local * ctx_size
    head_count = model_width // head_size
    group_size = head_count // kv_count
    local_heads = head_count // ctx_size
    local_width = model_width // ctx_size
    kv_width = kv_count * head_size
    piece = kv_width // ctx_size
    copies = ctx_size // kv_count

    def per_owner(cache):
        picked = jnp.repeat(cache[0], copies, axis=2)
        return jnp.transpose(picked, (1, 2, 0, 3)).reshape(cache_local, ctx_size, -1)

    cache_rows = jnp.concatenate([per_owner(cached_keys), per_owner(cached_values)], axis=-1)

    forward_outs = []
    backward_outs = []
    for stretch in range(stretch_count):
        gain_row = norm_gain[0, stretch]
        key_rows = key_weight[0, stretch]
        value_rows = value_weight[0, stretch]
        forward_rows = forward_in[0, stretch]
        backward_rows = backward_in[0, stretch]
        grad_rows = grad_out[0, stretch]
        forward_acts = normalize(forward_rows, gain_row)[2]
        backward_acts = normalize(backward_rows, gain_row)[2]
        outgoing = [
            forward_acts.reshape(local_rows, ctx_size, local_width),
            backward_acts.reshape(local_rows, ctx_size, local_width),
            grad_rows.reshape(local_rows, ctx_size, local_width),
        ]
        if stretch == 0:
            outgoing.append(cache_rows)
        sent = lax.all_to_all(
            jnp.stack(outgoing), "ctx", split_axis=2, concat_axis=1, tiled=True
        )
        if stretch == 0:
            cache_heads = sent[3].reshape(cache_len, 2, stretch_count, head_size)
        forward_slice = sent[0].reshape(seg_len, local_width)
        backward_slice = sent[1].reshape(seg_len, local_width)
        grad_slice = sent[2].reshape(seg_len, local_width)
        both_slices = jnp.stack([forward_slice, backward_slice])
        partial_value = jnp.concatenate(
            [
                jnp.einsum("btf,fe->bte", both_slices, key_rows, preferred_element_type=jnp.float32),
                jnp.einsum("btf,fe->bte", both_slices, value_rows, preferred_element_type=jnp.float32),
            ]
        ).astype(jnp.bfloat16)
        new_kv = reduce_to_head(partial_value, rank_id, ctx_size).reshape(2, 2, seg_len, head_size)
        new_kv = jnp.stack([new_kv[:, 0], new_kv[:, 1]], axis=0)
        cached_k = cache_heads[:, 0, stretch]
        cached_v = cache_heads[:, 1, stretch]
        forward_key_list = jnp.concatenate([cached_k, new_kv[0, 0]], axis=0)
        forward_value_list = jnp.concatenate([cached_v, new_kv[0, 1]], axis=0)
        backward_key_list = jnp.concatenate([cached_k, new_kv[1, 0]], axis=0)
        backward_value_list = jnp.concatenate([cached_v, new_kv[1, 1]], axis=0)
        attended = attend(
            forward_slice.reshape(seg_len, local_heads, head_size),
            forward_key_list,
            forward_value_list,
            segment_index[0, stretch, 0],
            cache_len,
        )[2]
        grad_query, grad_key, grad_value = attend_back(
            backward_slice.reshape(seg_len, local_heads, head_size),
            backward_key_list,
            backward_value_list,
            segment_index[0, stretch, 1],
            cache_len,
            grad_slice.reshape(seg_len, local_heads, head_size),
        )
        run_sums = jnp.stack([grad_key, grad_value])
        other_run = swapped_pairs(run_sums, "ctx")
        head_grads = (run_sums.astype(jnp.float32) + other_run.astype(jnp.float32)).astype(
            jnp.bfloat16
        )
        half_rows = seg_len // 2
        my_half = lax.dynamic_slice_in_dim(head_grads, (rank_id % 2) * half_rows, half_rows, 1)
        every_half = lax.all_gather(my_half, "ctx", axis=0, tiled=False)
        every_half = every_half.reshape(kv_count, 2, 2, half_rows, head_size)
        key_rows_heads = key_rows.reshape(local_width, kv_count, head_size)
        value_rows_heads = value_rows.reshape(local_width, kv_count, head_size)
        back_rows = jnp.einsum(
            "jhtd,fjd->htf", every_half[:, :, 0], key_rows_heads, preferred_element_type=jnp.float32
        )
        back_rows = back_rows + jnp.einsum(
            "jhtd,fjd->htf",
            every_half[:, :, 1],
            value_rows_heads,
            preferred_element_type=jnp.float32,
        )
        grad_acts = (
            grad_query.reshape(seg_len, -1).astype(jnp.float32) + back_rows.reshape(seg_len, -1)
        ).astype(jnp.bfloat16)
        returned = lax.all_to_all(
            jnp.stack([attended.reshape(ctx_size, local_rows, -1), grad_acts.reshape(ctx_size, local_rows, -1)]),
            "ctx",
            split_axis=1,
            concat_axis=3,
            tiled=True,
        )
        attn_rows = returned[0].reshape(local_rows, model_width)
        section_out = (forward_rows.astype(jnp.float32) + attn_rows.astype(jnp.float32)).astype(
            jnp.bfloat16
        )
        section_grad = input_grad(
            backward_rows, gain_row, returned[1].reshape(local_rows, model_width), grad_rows
        )
        forward_outs.append(passed_along(section_out, "pipe", 1))
        backward_outs.append(passed_along(section_grad, "pipe", -1))
    pipe_rank = lax.axis_index("pipe")
    arrived = jnp.stack(forward_outs)
    next_forward = jnp.where(pipe_rank == 0, jnp.roll(arrived, 1, axis=0), arrived)
    came_back = jnp.stack(backward_outs)
    next_backward = jnp.where(
        pipe_rank == lax.axis_size("pipe") - 1, jnp.roll(came_back, -1, axis=0), came_back
    )
    return (next_forward[None], next_backward[None])


def solution(mesh):
    in_specs = (
        P("pipe", None, "ctx", None),
        P("pipe", None, "ctx", None),
        P("pipe", None, "ctx", None),
        P("pipe", None, "ctx", None, None),
        P("pipe", None, "ctx", None, None),
        P("pipe", None, None),
        P("pipe", None, "ctx", None),
        P("pipe", None, "ctx", None),
        P("pipe", None, None),
    )
    out_specs = (P("pipe", None, "ctx", None), P("pipe", None, "ctx", None))
    return jax.shard_map(
        on_device, mesh=mesh, in_specs=in_specs, out_specs=out_specs, check_vma=False
    )
```

```python
import jax
import jax.numpy as jnp
from jax import lax
from jax.sharding import PartitionSpec as P

NEGATIVE = -1e30


def passed_along(array, axis, by):
    count = lax.axis_size(axis)
    return lax.ppermute(array, axis, [(i, (i + by) % count) for i in range(count)])


def swapped_pairs(array, axis):
    count = lax.axis_size(axis)
    return lax.ppermute(array, axis, [(i, i ^ 1) for i in range(count)])


def swapped_with(array, axis, mask):
    count = lax.axis_size(axis)
    return lax.ppermute(array, axis, [(i, i ^ mask) for i in range(count)])


def reduce_to_head(partial, rank_id, ctx_size):
    rows = partial.shape[1]
    core = rank_id % 2
    half = rows // 2
    kept = lax.dynamic_slice_in_dim(partial, core * half, half, 1)
    given = lax.dynamic_slice_in_dim(partial, (1 - core) * half, half, 1)
    total = kept.astype(jnp.float32) + swapped_with(given, "ctx", 1).astype(jnp.float32)
    mask = ctx_size // 2
    while mask > 1:
        bit = (rank_id // mask) % 2
        width = total.shape[2] // 2
        kept = lax.dynamic_slice_in_dim(total, bit * width, width, 2)
        given = lax.dynamic_slice_in_dim(total, (1 - bit) * width, width, 2)
        total = kept + swapped_with(given.astype(jnp.bfloat16), "ctx", mask).astype(jnp.float32)
        mask //= 2
    mine = total.astype(jnp.bfloat16)
    theirs = swapped_with(mine, "ctx", 1)
    return jnp.where(
        core == 0,
        jnp.concatenate([mine, theirs], axis=1),
        jnp.concatenate([theirs, mine], axis=1),
    )


def normalize(in_rows, gain_row):
    as_float = in_rows.astype(jnp.float32)
    inverse = lax.rsqrt(jnp.mean(as_float * as_float, axis=-1, keepdims=True) + 1e-05)
    normed = as_float * inverse
    return (normed, inverse, (normed * gain_row).astype(jnp.bfloat16))


def probabilities(queries, key_list, position, cache_len):
    seg_len = queries.shape[0]
    factor = queries.shape[-1] ** (-0.5)
    scores = (
        jnp.einsum("tgd,sd->gts", queries, key_list, preferred_element_type=jnp.float32) * factor
    )
    column = lax.broadcasted_iota(jnp.int32, (seg_len, key_list.shape[0]), 1)
    row_ids = lax.broadcasted_iota(jnp.int32, (seg_len, key_list.shape[0]), 0)
    visible = jnp.where(
        column < cache_len, column < position * seg_len, column - cache_len <= row_ids
    )
    scores = jnp.where(visible, scores, NEGATIVE)
    row_max = jnp.max(scores, axis=-1, keepdims=True)
    lifted = jnp.exp(scores - row_max)
    return lifted / jnp.sum(lifted, axis=-1, keepdims=True)


def attend(queries, key_list, value_list, position, cache_len):
    prob_full = probabilities(queries, key_list, position, cache_len)
    prob_half = prob_full.astype(jnp.bfloat16)
    attended = jnp.einsum(
        "gts,sd->tgd", prob_half, value_list, preferred_element_type=jnp.float32
    )
    return (prob_full, prob_half, attended.astype(jnp.bfloat16))


def attend_back(queries, key_list, value_list, position, cache_len, grad_heads):
    prob_full, prob_half, attended = attend(queries, key_list, value_list, position, cache_len)
    grad_prob = jnp.einsum(
        "tgd,sd->gts", grad_heads, value_list, preferred_element_type=jnp.float32
    )
    row_delta = jnp.sum(grad_heads.astype(jnp.float32) * attended.astype(jnp.float32), axis=-1)
    row_delta = jnp.transpose(row_delta, (1, 0))[..., None]
    factor = queries.shape[-1] ** (-0.5)
    grad_score = (prob_full * (grad_prob - row_delta) * factor).astype(jnp.bfloat16)
    grad_query = jnp.einsum(
        "gts,sd->tgd", grad_score, key_list, preferred_element_type=jnp.float32
    ).astype(jnp.bfloat16)
    grad_key = jnp.einsum(
        "gts,tgd->sd", grad_score[..., cache_len:], queries, preferred_element_type=jnp.float32
    )
    grad_value = jnp.einsum(
        "gts,tgd->sd", prob_half[..., cache_len:], grad_heads, preferred_element_type=jnp.float32
    )
    return (grad_query, grad_key.astype(jnp.bfloat16), grad_value.astype(jnp.bfloat16))


def input_grad(in_rows, gain_row, grad_acts, grad_rows):
    parts = normalize(in_rows, gain_row)
    normed = parts[0]
    inverse = parts[1]
    grad_normed = grad_acts.astype(jnp.float32) * gain_row
    grad_input = inverse * (
        grad_normed - normed * jnp.mean(grad_normed * normed, axis=-1, keepdims=True)
    )
    return (grad_rows.astype(jnp.float32) + grad_input).astype(jnp.bfloat16)


def on_device(
    forward_in,
    backward_in,
    grad_out,
    cached_keys,
    cached_values,
    norm_gain,
    key_weight,
    value_weight,
    segment_index,
):
    ctx_size = lax.axis_size("ctx")
    rank_id = lax.axis_index("ctx")
    stretch_count = forward_in.shape[1]
    local_rows = forward_in.shape[2]
    model_width = forward_in.shape[3]
    kv_count = cached_keys.shape[3]
    head_size = cached_keys.shape[4]
    seg_len = local_rows * ctx_size
    cache_local = cached_keys.shape[2]
    cache_len = cache_local * ctx_size
    head_count = model_width // head_size
    group_size = head_count // kv_count
    local_heads = head_count // ctx_size
    local_width = model_width // ctx_size
    kv_width = kv_count * head_size
    piece = kv_width // ctx_size
    copies = ctx_size // kv_count

    def per_owner(cache):
        picked = jnp.repeat(cache[0], copies, axis=2)
        return jnp.transpose(picked, (1, 2, 0, 3)).reshape(cache_local, ctx_size, -1)

    cache_rows = jnp.concatenate([per_owner(cached_keys), per_owner(cached_values)], axis=-1)

    forward_outs = []
    backward_outs = []
    for stretch in range(stretch_count):
        gain_row = norm_gain[0, stretch]
        key_rows = key_weight[0, stretch]
        value_rows = value_weight[0, stretch]
        forward_rows = forward_in[0, stretch]
        backward_rows = backward_in[0, stretch]
        grad_rows = grad_out[0, stretch]
        forward_acts = normalize(forward_rows, gain_row)[2]
        backward_acts = normalize(backward_rows, gain_row)[2]
        outgoing = [
            forward_acts.reshape(local_rows, ctx_size, local_width),
            backward_acts.reshape(local_rows, ctx_size, local_width),
            grad_rows.reshape(local_rows, ctx_size, local_width),
        ]
        if stretch == 0:
            outgoing.append(cache_rows)
        outgoing = jnp.stack(outgoing)
        if stretch > 0:
            outgoing, _ = lax.optimization_barrier((outgoing, previous_sent))
        sent = lax.all_to_all(outgoing, "ctx", split_axis=2, concat_axis=1, tiled=True)
        previous_sent = sent
        if stretch == 0:
            cache_heads = sent[3].reshape(cache_len, 2, stretch_count, head_size)
        forward_slice = sent[0].reshape(seg_len, local_width)
        backward_slice = sent[1].reshape(seg_len, local_width)
        grad_slice = sent[2].reshape(seg_len, local_width)
        both_slices = jnp.stack([forward_slice, backward_slice])
        partial_value = jnp.concatenate(
            [
                jnp.einsum("btf,fe->bte", both_slices, key_rows, preferred_element_type=jnp.float32),
                jnp.einsum("btf,fe->bte", both_slices, value_rows, preferred_element_type=jnp.float32),
            ]
        ).astype(jnp.bfloat16)
        if stretch > 0:
            partial_value, _ = lax.optimization_barrier((partial_value, previous_kv))
        new_kv = reduce_to_head(partial_value, rank_id, ctx_size).reshape(2, 2, seg_len, head_size)
        previous_kv = new_kv
        new_kv = jnp.stack([new_kv[:, 0], new_kv[:, 1]], axis=0)
        cached_k = cache_heads[:, 0, stretch]
        cached_v = cache_heads[:, 1, stretch]
        forward_key_list = jnp.concatenate([cached_k, new_kv[0, 0]], axis=0)
        forward_value_list = jnp.concatenate([cached_v, new_kv[0, 1]], axis=0)
        backward_key_list = jnp.concatenate([cached_k, new_kv[1, 0]], axis=0)
        backward_value_list = jnp.concatenate([cached_v, new_kv[1, 1]], axis=0)
        attended = attend(
            forward_slice.reshape(seg_len, local_heads, head_size),
            forward_key_list,
            forward_value_list,
            segment_index[0, stretch, 0],
            cache_len,
        )[2]
        grad_query, grad_key, grad_value = attend_back(
            backward_slice.reshape(seg_len, local_heads, head_size),
            backward_key_list,
            backward_value_list,
            segment_index[0, stretch, 1],
            cache_len,
            grad_slice.reshape(seg_len, local_heads, head_size),
        )
        run_sums = jnp.stack([grad_key, grad_value])
        other_run = swapped_pairs(run_sums, "ctx")
        head_grads = (run_sums.astype(jnp.float32) + other_run.astype(jnp.float32)).astype(
            jnp.bfloat16
        )
        half_rows = seg_len // 2
        my_half = lax.dynamic_slice_in_dim(head_grads, (rank_id % 2) * half_rows, half_rows, 1)
        every_half = lax.all_gather(my_half, "ctx", axis=0, tiled=False)
        every_half = every_half.reshape(kv_count, 2, 2, half_rows, head_size)
        key_rows_heads = key_rows.reshape(local_width, kv_count, head_size)
        value_rows_heads = value_rows.reshape(local_width, kv_count, head_size)
        back_rows = jnp.einsum(
            "jhtd,fjd->htf", every_half[:, :, 0], key_rows_heads, preferred_element_type=jnp.float32
        )
        back_rows = back_rows + jnp.einsum(
            "jhtd,fjd->htf",
            every_half[:, :, 1],
            value_rows_heads,
            preferred_element_type=jnp.float32,
        )
        grad_acts = (
            grad_query.reshape(seg_len, -1).astype(jnp.float32) + back_rows.reshape(seg_len, -1)
        ).astype(jnp.bfloat16)
        returned = lax.all_to_all(
            jnp.stack([attended.reshape(ctx_size, local_rows, -1), grad_acts.reshape(ctx_size, local_rows, -1)]),
            "ctx",
            split_axis=1,
            concat_axis=3,
            tiled=True,
        )
        attn_rows = returned[0].reshape(local_rows, model_width)
        section_out = (forward_rows.astype(jnp.float32) + attn_rows.astype(jnp.float32)).astype(
            jnp.bfloat16
        )
        section_grad = input_grad(
            backward_rows, gain_row, returned[1].reshape(local_rows, model_width), grad_rows
        )
        forward_outs.append(passed_along(section_out, "pipe", 1))
        backward_outs.append(passed_along(section_grad, "pipe", -1))
    pipe_rank = lax.axis_index("pipe")
    arrived = jnp.stack(forward_outs)
    next_forward = jnp.where(pipe_rank == 0, jnp.roll(arrived, 1, axis=0), arrived)
    came_back = jnp.stack(backward_outs)
    next_backward = jnp.where(
        pipe_rank == lax.axis_size("pipe") - 1, jnp.roll(came_back, -1, axis=0), came_back
    )
    return (next_forward[None], next_backward[None])


def solution(mesh):
    in_specs = (
        P("pipe", None, "ctx", None),
        P("pipe", None, "ctx", None),
        P("pipe", None, "ctx", None),
        P("pipe", None, "ctx", None, None),
        P("pipe", None, "ctx", None, None),
        P("pipe", None, None),
        P("pipe", None, "ctx", None),
        P("pipe", None, "ctx", None),
        P("pipe", None, None),
    )
    out_specs = (P("pipe", None, "ctx", None), P("pipe", None, "ctx", None))
    return jax.shard_map(
        on_device, mesh=mesh, in_specs=in_specs, out_specs=out_specs, check_vma=False
    )
```

```python
import jax
import jax.numpy as jnp
from jax import lax
from jax.sharding import PartitionSpec as P

NEGATIVE = -1e30


def passed_along(array, axis, by):
    count = lax.axis_size(axis)
    return lax.ppermute(array, axis, [(i, (i + by) % count) for i in range(count)])


def swapped_pairs(array, axis):
    count = lax.axis_size(axis)
    return lax.ppermute(array, axis, [(i, i ^ 1) for i in range(count)])


def swapped_with(array, axis, mask):
    count = lax.axis_size(axis)
    return lax.ppermute(array, axis, [(i, i ^ mask) for i in range(count)])


def reduce_to_head(partial, rank_id, ctx_size, orders):
    rows = partial.shape[1]
    core = rank_id % 2
    half = rows // 2
    kept = lax.dynamic_slice_in_dim(partial, core * half, half, 1)
    given = lax.dynamic_slice_in_dim(partial, (1 - core) * half, half, 1)
    total = kept.astype(jnp.float32) + swapped_with(given, "ctx", 1).astype(jnp.float32)
    group = half // len(orders)
    finished = []
    for index, order in enumerate(orders):
        part = total[:, index * group : (index + 1) * group]
        for mask in order:
            bit = (rank_id // mask) % 2
            width = part.shape[2] // 2
            kept = lax.dynamic_slice_in_dim(part, bit * width, width, 2)
            given = lax.dynamic_slice_in_dim(part, (1 - bit) * width, width, 2)
            part = kept + swapped_with(given.astype(jnp.bfloat16), "ctx", mask).astype(jnp.float32)
        finished.append(part)
    mine = jnp.concatenate(finished, axis=1).astype(jnp.bfloat16)
    theirs = swapped_with(mine, "ctx", 1)
    return jnp.where(
        core == 0,
        jnp.concatenate([mine, theirs], axis=1),
        jnp.concatenate([theirs, mine], axis=1),
    )


def column_order(weight, order, head_size):
    bits = len(order)
    natural = sorted(order, reverse=True)
    split = weight.reshape(weight.shape[:-1] + (2,) * bits + (head_size,))
    lead = weight.ndim - 1
    axes = list(range(lead)) + [lead + natural.index(m) for m in order] + [lead + bits]
    return jnp.transpose(split, axes).reshape(weight.shape)


def normalize(in_rows, gain_row):
    as_float = in_rows.astype(jnp.float32)
    inverse = lax.rsqrt(jnp.mean(as_float * as_float, axis=-1, keepdims=True) + 1e-05)
    normed = as_float * inverse
    return (normed, inverse, (normed * gain_row).astype(jnp.bfloat16))


def probabilities(queries, key_list, position, cache_len):
    seg_len = queries.shape[0]
    factor = queries.shape[-1] ** (-0.5)
    scores = (
        jnp.einsum("tgd,sd->gts", queries, key_list, preferred_element_type=jnp.float32) * factor
    )
    column = lax.broadcasted_iota(jnp.int32, (seg_len, key_list.shape[0]), 1)
    row_ids = lax.broadcasted_iota(jnp.int32, (seg_len, key_list.shape[0]), 0)
    visible = jnp.where(
        column < cache_len, column < position * seg_len, column - cache_len <= row_ids
    )
    scores = jnp.where(visible, scores, NEGATIVE)
    row_max = jnp.max(scores, axis=-1, keepdims=True)
    lifted = jnp.exp(scores - row_max)
    return lifted / jnp.sum(lifted, axis=-1, keepdims=True)


def attend(queries, key_list, value_list, position, cache_len):
    prob_full = probabilities(queries, key_list, position, cache_len)
    prob_half = prob_full.astype(jnp.bfloat16)
    attended = jnp.einsum(
        "gts,sd->tgd", prob_half, value_list, preferred_element_type=jnp.float32
    )
    return (prob_full, prob_half, attended.astype(jnp.bfloat16))


def attend_back(queries, key_list, value_list, position, cache_len, grad_heads):
    prob_full, prob_half, attended = attend(queries, key_list, value_list, position, cache_len)
    grad_prob = jnp.einsum(
        "tgd,sd->gts", grad_heads, value_list, preferred_element_type=jnp.float32
    )
    row_delta = jnp.sum(grad_heads.astype(jnp.float32) * attended.astype(jnp.float32), axis=-1)
    row_delta = jnp.transpose(row_delta, (1, 0))[..., None]
    factor = queries.shape[-1] ** (-0.5)
    grad_score = (prob_full * (grad_prob - row_delta) * factor).astype(jnp.bfloat16)
    grad_query = jnp.einsum(
        "gts,sd->tgd", grad_score, key_list, preferred_element_type=jnp.float32
    ).astype(jnp.bfloat16)
    grad_key = jnp.einsum(
        "gts,tgd->sd", grad_score[..., cache_len:], queries, preferred_element_type=jnp.float32
    )
    grad_value = jnp.einsum(
        "gts,tgd->sd", prob_half[..., cache_len:], grad_heads, preferred_element_type=jnp.float32
    )
    return (grad_query, grad_key.astype(jnp.bfloat16), grad_value.astype(jnp.bfloat16))


def input_grad(in_rows, gain_row, grad_acts, grad_rows):
    parts = normalize(in_rows, gain_row)
    normed = parts[0]
    inverse = parts[1]
    grad_normed = grad_acts.astype(jnp.float32) * gain_row
    grad_input = inverse * (
        grad_normed - normed * jnp.mean(grad_normed * normed, axis=-1, keepdims=True)
    )
    return (grad_rows.astype(jnp.float32) + grad_input).astype(jnp.bfloat16)


def on_device(
    forward_in,
    backward_in,
    grad_out,
    cached_keys,
    cached_values,
    norm_gain,
    key_weight,
    value_weight,
    segment_index,
):
    ctx_size = lax.axis_size("ctx")
    rank_id = lax.axis_index("ctx")
    stretch_count = forward_in.shape[1]
    local_rows = forward_in.shape[2]
    model_width = forward_in.shape[3]
    kv_count = cached_keys.shape[3]
    head_size = cached_keys.shape[4]
    seg_len = local_rows * ctx_size
    cache_local = cached_keys.shape[2]
    cache_len = cache_local * ctx_size
    head_count = model_width // head_size
    group_size = head_count // kv_count
    local_heads = head_count // ctx_size
    local_width = model_width // ctx_size
    kv_width = kv_count * head_size
    piece = kv_width // ctx_size
    copies = ctx_size // kv_count
    masks = []
    mask = ctx_size // 2
    while mask > 1:
        masks.append(mask)
        mask //= 2
    orders = (tuple(masks), (masks[-1],) + tuple(masks[:-1]))

    def per_owner(cache):
        picked = jnp.repeat(cache[0], copies, axis=2)
        return jnp.transpose(picked, (1, 2, 0, 3)).reshape(cache_local, ctx_size, -1)

    cache_rows = jnp.concatenate([per_owner(cached_keys), per_owner(cached_values)], axis=-1)

    forward_outs = []
    backward_outs = []
    for stretch in range(stretch_count):
        gain_row = norm_gain[0, stretch]
        key_rows = key_weight[0, stretch]
        value_rows = value_weight[0, stretch]
        forward_rows = forward_in[0, stretch]
        backward_rows = backward_in[0, stretch]
        grad_rows = grad_out[0, stretch]
        forward_acts = normalize(forward_rows, gain_row)[2]
        backward_acts = normalize(backward_rows, gain_row)[2]
        outgoing = [
            forward_acts.reshape(local_rows, ctx_size, local_width),
            backward_acts.reshape(local_rows, ctx_size, local_width),
            grad_rows.reshape(local_rows, ctx_size, local_width),
        ]
        if stretch == 0:
            outgoing.append(cache_rows)
        sent = lax.all_to_all(
            jnp.stack(outgoing), "ctx", split_axis=2, concat_axis=1, tiled=True
        )
        if stretch == 0:
            cache_heads = sent[3].reshape(cache_len, 2, stretch_count, head_size)
        forward_slice = sent[0].reshape(seg_len, local_width)
        backward_slice = sent[1].reshape(seg_len, local_width)
        grad_slice = sent[2].reshape(seg_len, local_width)
        both_slices = jnp.stack([forward_slice, backward_slice])
        group_rows = both_slices.reshape(2, 2, len(orders), -1, local_width)
        partial_value = jnp.stack(
            [
                jnp.stack(
                    [
                        jnp.einsum(
                            "btf,fe->bte",
                            group_rows[:, :, index].reshape(2, -1, local_width),
                            column_order(rows_weight, order, head_size),
                            preferred_element_type=jnp.float32,
                        ).reshape(2, 2, -1, kv_width)
                        for index, order in enumerate(orders)
                    ],
                    axis=2,
                )
                for rows_weight in (key_rows, value_rows)
            ]
        ).astype(jnp.bfloat16).reshape(4, seg_len, kv_width)
        new_kv = reduce_to_head(partial_value, rank_id, ctx_size, orders).reshape(
            2, 2, seg_len, head_size
        )
        new_kv = jnp.stack([new_kv[:, 0], new_kv[:, 1]], axis=0)
        cached_k = cache_heads[:, 0, stretch]
        cached_v = cache_heads[:, 1, stretch]
        forward_key_list = jnp.concatenate([cached_k, new_kv[0, 0]], axis=0)
        forward_value_list = jnp.concatenate([cached_v, new_kv[0, 1]], axis=0)
        backward_key_list = jnp.concatenate([cached_k, new_kv[1, 0]], axis=0)
        backward_value_list = jnp.concatenate([cached_v, new_kv[1, 1]], axis=0)
        attended = attend(
            forward_slice.reshape(seg_len, local_heads, head_size),
            forward_key_list,
            forward_value_list,
            segment_index[0, stretch, 0],
            cache_len,
        )[2]
        grad_query, grad_key, grad_value = attend_back(
            backward_slice.reshape(seg_len, local_heads, head_size),
            backward_key_list,
            backward_value_list,
            segment_index[0, stretch, 1],
            cache_len,
            grad_slice.reshape(seg_len, local_heads, head_size),
        )
        run_sums = jnp.stack([grad_key, grad_value])
        other_run = swapped_pairs(run_sums, "ctx")
        head_grads = (run_sums.astype(jnp.float32) + other_run.astype(jnp.float32)).astype(
            jnp.bfloat16
        )
        half_rows = seg_len // 2
        my_half = lax.dynamic_slice_in_dim(head_grads, (rank_id % 2) * half_rows, half_rows, 1)
        every_half = lax.all_gather(my_half, "ctx", axis=0, tiled=False)
        every_half = every_half.reshape(kv_count, 2, 2, half_rows, head_size)
        key_rows_heads = key_rows.reshape(local_width, kv_count, head_size)
        value_rows_heads = value_rows.reshape(local_width, kv_count, head_size)
        back_rows = jnp.einsum(
            "jhtd,fjd->htf", every_half[:, :, 0], key_rows_heads, preferred_element_type=jnp.float32
        )
        back_rows = back_rows + jnp.einsum(
            "jhtd,fjd->htf",
            every_half[:, :, 1],
            value_rows_heads,
            preferred_element_type=jnp.float32,
        )
        grad_acts = (
            grad_query.reshape(seg_len, -1).astype(jnp.float32) + back_rows.reshape(seg_len, -1)
        ).astype(jnp.bfloat16)
        returned = lax.all_to_all(
            jnp.stack([attended.reshape(ctx_size, local_rows, -1), grad_acts.reshape(ctx_size, local_rows, -1)]),
            "ctx",
            split_axis=1,
            concat_axis=3,
            tiled=True,
        )
        attn_rows = returned[0].reshape(local_rows, model_width)
        section_out = (forward_rows.astype(jnp.float32) + attn_rows.astype(jnp.float32)).astype(
            jnp.bfloat16
        )
        section_grad = input_grad(
            backward_rows, gain_row, returned[1].reshape(local_rows, model_width), grad_rows
        )
        forward_outs.append(passed_along(section_out, "pipe", 1))
        backward_outs.append(passed_along(section_grad, "pipe", -1))
    pipe_rank = lax.axis_index("pipe")
    arrived = jnp.stack(forward_outs)
    next_forward = jnp.where(pipe_rank == 0, jnp.roll(arrived, 1, axis=0), arrived)
    came_back = jnp.stack(backward_outs)
    next_backward = jnp.where(
        pipe_rank == lax.axis_size("pipe") - 1, jnp.roll(came_back, -1, axis=0), came_back
    )
    return (next_forward[None], next_backward[None])


def solution(mesh):
    in_specs = (
        P("pipe", None, "ctx", None),
        P("pipe", None, "ctx", None),
        P("pipe", None, "ctx", None),
        P("pipe", None, "ctx", None, None),
        P("pipe", None, "ctx", None, None),
        P("pipe", None, None),
        P("pipe", None, "ctx", None),
        P("pipe", None, "ctx", None),
        P("pipe", None, None),
    )
    out_specs = (P("pipe", None, "ctx", None), P("pipe", None, "ctx", None))
    return jax.shard_map(
        on_device, mesh=mesh, in_specs=in_specs, out_specs=out_specs, check_vma=False
    )
```

```python
import jax
import jax.numpy as jnp
from jax import lax
from jax.sharding import PartitionSpec as P

NEGATIVE = -1e30


def passed_along(array, axis, by):
    count = lax.axis_size(axis)
    return lax.ppermute(array, axis, [(i, (i + by) % count) for i in range(count)])


def swapped_pairs(array, axis):
    count = lax.axis_size(axis)
    return lax.ppermute(array, axis, [(i, i ^ 1) for i in range(count)])


def swapped_with(array, axis, mask):
    count = lax.axis_size(axis)
    return lax.ppermute(array, axis, [(i, i ^ mask) for i in range(count)])


def reduce_to_head(partial, rank_id, ctx_size, orders):
    rows = partial.shape[1]
    core = rank_id % 2
    half = rows // 2
    kept = lax.dynamic_slice_in_dim(partial, core * half, half, 1)
    given = lax.dynamic_slice_in_dim(partial, (1 - core) * half, half, 1)
    total = kept.astype(jnp.float32) + swapped_with(given, "ctx", 1).astype(jnp.float32)
    group = half // len(orders)
    finished = []
    for index, order in enumerate(orders):
        part = total[:, index * group : (index + 1) * group]
        for mask in order:
            bit = (rank_id // mask) % 2
            width = part.shape[2] // 2
            kept = lax.dynamic_slice_in_dim(part, bit * width, width, 2)
            given = lax.dynamic_slice_in_dim(part, (1 - bit) * width, width, 2)
            part = kept + swapped_with(given.astype(jnp.bfloat16), "ctx", mask).astype(jnp.float32)
        finished.append(part)
    mine = jnp.concatenate(finished, axis=1).astype(jnp.bfloat16)
    theirs = swapped_with(mine, "ctx", 1)
    return jnp.where(
        core == 0,
        jnp.concatenate([mine, theirs], axis=1),
        jnp.concatenate([theirs, mine], axis=1),
    )


def gather_heads(head_grads, rank_id, ctx_size):
    core = rank_id % 2
    rows = head_grads.shape[1]
    half = rows // 2
    held = lax.dynamic_slice_in_dim(head_grads, core * half, half, 1)[None]
    mask = 2
    while mask < ctx_size:
        other = swapped_with(held, "ctx", mask)
        bit = (rank_id // mask) % 2
        held = jnp.where(
            bit == 0,
            jnp.concatenate([held, other], axis=0),
            jnp.concatenate([other, held], axis=0),
        )
        mask *= 2
    other = swapped_with(held, "ctx", 1)
    return jnp.where(
        core == 0,
        jnp.concatenate([held, other], axis=2),
        jnp.concatenate([other, held], axis=2),
    )


def column_order(weight, order, head_size):
    bits = len(order)
    natural = sorted(order, reverse=True)
    split = weight.reshape(weight.shape[:-1] + (2,) * bits + (head_size,))
    lead = weight.ndim - 1
    axes = list(range(lead)) + [lead + natural.index(m) for m in order] + [lead + bits]
    return jnp.transpose(split, axes).reshape(weight.shape)


def normalize(in_rows, gain_row):
    as_float = in_rows.astype(jnp.float32)
    inverse = lax.rsqrt(jnp.mean(as_float * as_float, axis=-1, keepdims=True) + 1e-05)
    normed = as_float * inverse
    return (normed, inverse, (normed * gain_row).astype(jnp.bfloat16))


def probabilities(queries, key_list, position, cache_len):
    seg_len = queries.shape[0]
    factor = queries.shape[-1] ** (-0.5)
    scores = (
        jnp.einsum("tgd,sd->gts", queries, key_list, preferred_element_type=jnp.float32) * factor
    )
    column = lax.broadcasted_iota(jnp.int32, (seg_len, key_list.shape[0]), 1)
    row_ids = lax.broadcasted_iota(jnp.int32, (seg_len, key_list.shape[0]), 0)
    visible = jnp.where(
        column < cache_len, column < position * seg_len, column - cache_len <= row_ids
    )
    scores = jnp.where(visible, scores, NEGATIVE)
    row_max = jnp.max(scores, axis=-1, keepdims=True)
    lifted = jnp.exp(scores - row_max)
    return lifted / jnp.sum(lifted, axis=-1, keepdims=True)


def attend(queries, key_list, value_list, position, cache_len):
    prob_full = probabilities(queries, key_list, position, cache_len)
    prob_half = prob_full.astype(jnp.bfloat16)
    attended = jnp.einsum(
        "gts,sd->tgd", prob_half, value_list, preferred_element_type=jnp.float32
    )
    return (prob_full, prob_half, attended.astype(jnp.bfloat16))


def attend_back(queries, key_list, value_list, position, cache_len, grad_heads):
    prob_full, prob_half, attended = attend(queries, key_list, value_list, position, cache_len)
    grad_prob = jnp.einsum(
        "tgd,sd->gts", grad_heads, value_list, preferred_element_type=jnp.float32
    )
    row_delta = jnp.sum(grad_heads.astype(jnp.float32) * attended.astype(jnp.float32), axis=-1)
    row_delta = jnp.transpose(row_delta, (1, 0))[..., None]
    factor = queries.shape[-1] ** (-0.5)
    grad_score = (prob_full * (grad_prob - row_delta) * factor).astype(jnp.bfloat16)
    grad_query = jnp.einsum(
        "gts,sd->tgd", grad_score, key_list, preferred_element_type=jnp.float32
    ).astype(jnp.bfloat16)
    grad_key = jnp.einsum(
        "gts,tgd->sd", grad_score[..., cache_len:], queries, preferred_element_type=jnp.float32
    )
    grad_value = jnp.einsum(
        "gts,tgd->sd", prob_half[..., cache_len:], grad_heads, preferred_element_type=jnp.float32
    )
    return (grad_query, grad_key.astype(jnp.bfloat16), grad_value.astype(jnp.bfloat16))


def input_grad(in_rows, gain_row, grad_acts, grad_rows):
    parts = normalize(in_rows, gain_row)
    normed = parts[0]
    inverse = parts[1]
    grad_normed = grad_acts.astype(jnp.float32) * gain_row
    grad_input = inverse * (
        grad_normed - normed * jnp.mean(grad_normed * normed, axis=-1, keepdims=True)
    )
    return (grad_rows.astype(jnp.float32) + grad_input).astype(jnp.bfloat16)


def on_device(
    forward_in,
    backward_in,
    grad_out,
    cached_keys,
    cached_values,
    norm_gain,
    key_weight,
    value_weight,
    segment_index,
):
    ctx_size = lax.axis_size("ctx")
    rank_id = lax.axis_index("ctx")
    stretch_count = forward_in.shape[1]
    local_rows = forward_in.shape[2]
    model_width = forward_in.shape[3]
    kv_count = cached_keys.shape[3]
    head_size = cached_keys.shape[4]
    seg_len = local_rows * ctx_size
    cache_local = cached_keys.shape[2]
    cache_len = cache_local * ctx_size
    head_count = model_width // head_size
    group_size = head_count // kv_count
    local_heads = head_count // ctx_size
    local_width = model_width // ctx_size
    kv_width = kv_count * head_size
    piece = kv_width // ctx_size
    copies = ctx_size // kv_count
    masks = []
    mask = ctx_size // 2
    while mask > 1:
        masks.append(mask)
        mask //= 2
    orders = (tuple(masks), (masks[-1],) + tuple(masks[:-1]))

    def per_owner(cache):
        picked = jnp.repeat(cache[0], copies, axis=2)
        return jnp.transpose(picked, (1, 2, 0, 3)).reshape(cache_local, ctx_size, -1)

    cache_rows = jnp.concatenate([per_owner(cached_keys), per_owner(cached_values)], axis=-1)

    forward_outs = []
    backward_outs = []
    for stretch in range(stretch_count):
        gain_row = norm_gain[0, stretch]
        key_rows = key_weight[0, stretch]
        value_rows = value_weight[0, stretch]
        forward_rows = forward_in[0, stretch]
        backward_rows = backward_in[0, stretch]
        grad_rows = grad_out[0, stretch]
        forward_acts = normalize(forward_rows, gain_row)[2]
        backward_acts = normalize(backward_rows, gain_row)[2]
        outgoing = [
            forward_acts.reshape(local_rows, ctx_size, local_width),
            backward_acts.reshape(local_rows, ctx_size, local_width),
            grad_rows.reshape(local_rows, ctx_size, local_width),
        ]
        if stretch == 0:
            outgoing.append(cache_rows)
        sent = lax.all_to_all(
            jnp.stack(outgoing), "ctx", split_axis=2, concat_axis=1, tiled=True
        )
        if stretch == 0:
            cache_heads = sent[3].reshape(cache_len, 2, stretch_count, head_size)
        forward_slice = sent[0].reshape(seg_len, local_width)
        backward_slice = sent[1].reshape(seg_len, local_width)
        grad_slice = sent[2].reshape(seg_len, local_width)
        both_slices = jnp.stack([forward_slice, backward_slice])
        group_rows = both_slices.reshape(2, 2, len(orders), -1, local_width)
        partial_value = jnp.stack(
            [
                jnp.stack(
                    [
                        jnp.einsum(
                            "btf,fe->bte",
                            group_rows[:, :, index].reshape(2, -1, local_width),
                            column_order(rows_weight, order, head_size),
                            preferred_element_type=jnp.float32,
                        ).reshape(2, 2, -1, kv_width)
                        for index, order in enumerate(orders)
                    ],
                    axis=2,
                )
                for rows_weight in (key_rows, value_rows)
            ]
        ).astype(jnp.bfloat16).reshape(4, seg_len, kv_width)
        new_kv = reduce_to_head(partial_value, rank_id, ctx_size, orders).reshape(
            2, 2, seg_len, head_size
        )
        new_kv = jnp.stack([new_kv[:, 0], new_kv[:, 1]], axis=0)
        cached_k = cache_heads[:, 0, stretch]
        cached_v = cache_heads[:, 1, stretch]
        forward_key_list = jnp.concatenate([cached_k, new_kv[0, 0]], axis=0)
        forward_value_list = jnp.concatenate([cached_v, new_kv[0, 1]], axis=0)
        backward_key_list = jnp.concatenate([cached_k, new_kv[1, 0]], axis=0)
        backward_value_list = jnp.concatenate([cached_v, new_kv[1, 1]], axis=0)
        attended = attend(
            forward_slice.reshape(seg_len, local_heads, head_size),
            forward_key_list,
            forward_value_list,
            segment_index[0, stretch, 0],
            cache_len,
        )[2]
        grad_query, grad_key, grad_value = attend_back(
            backward_slice.reshape(seg_len, local_heads, head_size),
            backward_key_list,
            backward_value_list,
            segment_index[0, stretch, 1],
            cache_len,
            grad_slice.reshape(seg_len, local_heads, head_size),
        )
        run_sums = jnp.stack([grad_key, grad_value])
        other_run = swapped_pairs(run_sums, "ctx")
        head_grads = (run_sums.astype(jnp.float32) + other_run.astype(jnp.float32)).astype(
            jnp.bfloat16
        )
        every_head = gather_heads(head_grads, rank_id, ctx_size)
        key_rows_heads = key_rows.reshape(local_width, kv_count, head_size)
        value_rows_heads = value_rows.reshape(local_width, kv_count, head_size)
        back_rows = jnp.einsum(
            "jtd,fjd->tf", every_head[:, 0], key_rows_heads, preferred_element_type=jnp.float32
        )
        back_rows = back_rows + jnp.einsum(
            "jtd,fjd->tf",
            every_head[:, 1],
            value_rows_heads,
            preferred_element_type=jnp.float32,
        )
        grad_acts = (
            grad_query.reshape(seg_len, -1).astype(jnp.float32) + back_rows.reshape(seg_len, -1)
        ).astype(jnp.bfloat16)
        returned = lax.all_to_all(
            jnp.stack([attended.reshape(ctx_size, local_rows, -1), grad_acts.reshape(ctx_size, local_rows, -1)]),
            "ctx",
            split_axis=1,
            concat_axis=3,
            tiled=True,
        )
        attn_rows = returned[0].reshape(local_rows, model_width)
        section_out = (forward_rows.astype(jnp.float32) + attn_rows.astype(jnp.float32)).astype(
            jnp.bfloat16
        )
        section_grad = input_grad(
            backward_rows, gain_row, returned[1].reshape(local_rows, model_width), grad_rows
        )
        forward_outs.append(passed_along(section_out, "pipe", 1))
        backward_outs.append(passed_along(section_grad, "pipe", -1))
    pipe_rank = lax.axis_index("pipe")
    arrived = jnp.stack(forward_outs)
    next_forward = jnp.where(pipe_rank == 0, jnp.roll(arrived, 1, axis=0), arrived)
    came_back = jnp.stack(backward_outs)
    next_backward = jnp.where(
        pipe_rank == lax.axis_size("pipe") - 1, jnp.roll(came_back, -1, axis=0), came_back
    )
    return (next_forward[None], next_backward[None])


def solution(mesh):
    in_specs = (
        P("pipe", None, "ctx", None),
        P("pipe", None, "ctx", None),
        P("pipe", None, "ctx", None),
        P("pipe", None, "ctx", None, None),
        P("pipe", None, "ctx", None, None),
        P("pipe", None, None),
        P("pipe", None, "ctx", None),
        P("pipe", None, "ctx", None),
        P("pipe", None, None),
    )
    out_specs = (P("pipe", None, "ctx", None), P("pipe", None, "ctx", None))
    return jax.shard_map(
        on_device, mesh=mesh, in_specs=in_specs, out_specs=out_specs, check_vma=False
    )
```

```python
import jax
import jax.numpy as jnp
from jax import lax
from jax.sharding import PartitionSpec as P

NEGATIVE = -1e30


def passed_along(array, axis, by):
    count = lax.axis_size(axis)
    return lax.ppermute(array, axis, [(i, (i + by) % count) for i in range(count)])


def swapped_pairs(array, axis):
    count = lax.axis_size(axis)
    return lax.ppermute(array, axis, [(i, i ^ 1) for i in range(count)])


def swapped_with(array, axis, mask):
    count = lax.axis_size(axis)
    return lax.ppermute(array, axis, [(i, i ^ mask) for i in range(count)])


def reduce_to_head(partial, rank_id, ctx_size, orders):
    rows = partial.shape[1]
    core = rank_id % 2
    half = rows // 2
    kept = lax.dynamic_slice_in_dim(partial, core * half, half, 1)
    given = lax.dynamic_slice_in_dim(partial, (1 - core) * half, half, 1)
    total = kept.astype(jnp.float32) + swapped_with(given, "ctx", 1).astype(jnp.float32)
    group = half // len(orders)
    finished = []
    for index, order in enumerate(orders):
        part = total[:, index * group : (index + 1) * group]
        for mask in order:
            bit = (rank_id // mask) % 2
            width = part.shape[2] // 2
            kept = lax.dynamic_slice_in_dim(part, bit * width, width, 2)
            given = lax.dynamic_slice_in_dim(part, (1 - bit) * width, width, 2)
            part = kept + swapped_with(given.astype(jnp.bfloat16), "ctx", mask).astype(jnp.float32)
        finished.append(part)
    mine = jnp.concatenate(finished, axis=1).astype(jnp.bfloat16)
    theirs = swapped_with(mine, "ctx", 1)
    return jnp.where(
        core == 0,
        jnp.concatenate([mine, theirs], axis=1),
        jnp.concatenate([theirs, mine], axis=1),
    )


def gather_heads(head_grads, rank_id, ctx_size):
    core = rank_id % 2
    rows = head_grads.shape[1]
    half = rows // 2
    held = lax.dynamic_slice_in_dim(head_grads, core * half, half, 1)[None]
    mask = 2
    while mask < ctx_size:
        other = swapped_with(held, "ctx", mask)
        bit = (rank_id // mask) % 2
        held = jnp.where(
            bit == 0,
            jnp.concatenate([held, other], axis=0),
            jnp.concatenate([other, held], axis=0),
        )
        mask *= 2
    other = swapped_with(held, "ctx", 1)
    return jnp.where(
        core == 0,
        jnp.concatenate([held, other], axis=2),
        jnp.concatenate([other, held], axis=2),
    )


def column_order(weight, order, head_size):
    natural = sorted(order, reverse=True)
    blocks = []
    for new_index in range(2 ** len(order)):
        old_index = 0
        for place, mask in enumerate(order):
            bit = (new_index >> (len(order) - 1 - place)) & 1
            old_index += bit << (len(order) - 1 - natural.index(mask))
        blocks.append(weight[..., old_index * head_size : (old_index + 1) * head_size])
    return jnp.concatenate(blocks, axis=-1)


def normalize(in_rows, gain_row):
    as_float = in_rows.astype(jnp.float32)
    inverse = lax.rsqrt(jnp.mean(as_float * as_float, axis=-1, keepdims=True) + 1e-05)
    normed = as_float * inverse
    return (normed, inverse, (normed * gain_row).astype(jnp.bfloat16))


def probabilities(queries, key_list, position, cache_len):
    seg_len = queries.shape[0]
    factor = queries.shape[-1] ** (-0.5)
    scores = (
        jnp.einsum("tgd,sd->gts", queries, key_list, preferred_element_type=jnp.float32) * factor
    )
    column = lax.broadcasted_iota(jnp.int32, (seg_len, key_list.shape[0]), 1)
    row_ids = lax.broadcasted_iota(jnp.int32, (seg_len, key_list.shape[0]), 0)
    visible = jnp.where(
        column < cache_len, column < position * seg_len, column - cache_len <= row_ids
    )
    scores = jnp.where(visible, scores, NEGATIVE)
    row_max = jnp.max(scores, axis=-1, keepdims=True)
    lifted = jnp.exp(scores - row_max)
    return lifted / jnp.sum(lifted, axis=-1, keepdims=True)


def attend(queries, key_list, value_list, position, cache_len):
    prob_full = probabilities(queries, key_list, position, cache_len)
    prob_half = prob_full.astype(jnp.bfloat16)
    attended = jnp.einsum(
        "gts,sd->tgd", prob_half, value_list, preferred_element_type=jnp.float32
    )
    return (prob_full, prob_half, attended.astype(jnp.bfloat16))


def attend_back(queries, key_list, value_list, position, cache_len, grad_heads):
    prob_full, prob_half, attended = attend(queries, key_list, value_list, position, cache_len)
    grad_prob = jnp.einsum(
        "tgd,sd->gts", grad_heads, value_list, preferred_element_type=jnp.float32
    )
    row_delta = jnp.sum(grad_heads.astype(jnp.float32) * attended.astype(jnp.float32), axis=-1)
    row_delta = jnp.transpose(row_delta, (1, 0))[..., None]
    factor = queries.shape[-1] ** (-0.5)
    grad_score = (prob_full * (grad_prob - row_delta) * factor).astype(jnp.bfloat16)
    grad_query = jnp.einsum(
        "gts,sd->tgd", grad_score, key_list, preferred_element_type=jnp.float32
    ).astype(jnp.bfloat16)
    grad_key = jnp.einsum(
        "gts,tgd->sd", grad_score[..., cache_len:], queries, preferred_element_type=jnp.float32
    )
    grad_value = jnp.einsum(
        "gts,tgd->sd", prob_half[..., cache_len:], grad_heads, preferred_element_type=jnp.float32
    )
    return (grad_query, grad_key.astype(jnp.bfloat16), grad_value.astype(jnp.bfloat16))


def input_grad(in_rows, gain_row, grad_acts, grad_rows):
    parts = normalize(in_rows, gain_row)
    normed = parts[0]
    inverse = parts[1]
    grad_normed = grad_acts.astype(jnp.float32) * gain_row
    grad_input = inverse * (
        grad_normed - normed * jnp.mean(grad_normed * normed, axis=-1, keepdims=True)
    )
    return (grad_rows.astype(jnp.float32) + grad_input).astype(jnp.bfloat16)


def on_device(
    forward_in,
    backward_in,
    grad_out,
    cached_keys,
    cached_values,
    norm_gain,
    key_weight,
    value_weight,
    segment_index,
):
    ctx_size = lax.axis_size("ctx")
    rank_id = lax.axis_index("ctx")
    stretch_count = forward_in.shape[1]
    local_rows = forward_in.shape[2]
    model_width = forward_in.shape[3]
    kv_count = cached_keys.shape[3]
    head_size = cached_keys.shape[4]
    seg_len = local_rows * ctx_size
    cache_local = cached_keys.shape[2]
    cache_len = cache_local * ctx_size
    head_count = model_width // head_size
    group_size = head_count // kv_count
    local_heads = head_count // ctx_size
    local_width = model_width // ctx_size
    kv_width = kv_count * head_size
    piece = kv_width // ctx_size
    copies = ctx_size // kv_count
    masks = []
    mask = ctx_size // 2
    while mask > 1:
        masks.append(mask)
        mask //= 2
    orders = (tuple(masks), (masks[-1],) + tuple(masks[:-1]))

    def per_owner(cache):
        picked = jnp.repeat(cache[0], copies, axis=2)
        return jnp.transpose(picked, (1, 2, 0, 3)).reshape(cache_local, ctx_size, -1)

    cache_rows = jnp.concatenate([per_owner(cached_keys), per_owner(cached_values)], axis=-1)

    forward_outs = []
    backward_outs = []
    for stretch in range(stretch_count):
        gain_row = norm_gain[0, stretch]
        key_rows = key_weight[0, stretch]
        value_rows = value_weight[0, stretch]
        forward_rows = forward_in[0, stretch]
        backward_rows = backward_in[0, stretch]
        grad_rows = grad_out[0, stretch]
        forward_acts = normalize(forward_rows, gain_row)[2]
        backward_acts = normalize(backward_rows, gain_row)[2]
        outgoing = [
            forward_acts.reshape(local_rows, ctx_size, local_width),
            backward_acts.reshape(local_rows, ctx_size, local_width),
            grad_rows.reshape(local_rows, ctx_size, local_width),
        ]
        if stretch == 0:
            outgoing.append(cache_rows)
        sent = lax.all_to_all(
            jnp.stack(outgoing), "ctx", split_axis=2, concat_axis=1, tiled=True
        )
        if stretch == 0:
            cache_heads = sent[3].reshape(cache_len, 2, stretch_count, head_size)
        forward_slice = sent[0].reshape(seg_len, local_width)
        backward_slice = sent[1].reshape(seg_len, local_width)
        grad_slice = sent[2].reshape(seg_len, local_width)
        both_slices = jnp.stack([forward_slice, backward_slice])
        group_rows = both_slices.reshape(2, 2, len(orders), -1, local_width)
        partial_value = jnp.stack(
            [
                jnp.stack(
                    [
                        jnp.einsum(
                            "btf,fe->bte",
                            group_rows[:, :, index].reshape(2, -1, local_width),
                            column_order(rows_weight, order, head_size),
                            preferred_element_type=jnp.float32,
                        ).reshape(2, 2, -1, kv_width)
                        for index, order in enumerate(orders)
                    ],
                    axis=2,
                )
                for rows_weight in (key_rows, value_rows)
            ]
        ).astype(jnp.bfloat16).reshape(4, seg_len, kv_width)
        new_kv = reduce_to_head(partial_value, rank_id, ctx_size, orders).reshape(
            2, 2, seg_len, head_size
        )
        new_kv = jnp.stack([new_kv[:, 0], new_kv[:, 1]], axis=0)
        cached_k = cache_heads[:, 0, stretch]
        cached_v = cache_heads[:, 1, stretch]
        forward_key_list = jnp.concatenate([cached_k, new_kv[0, 0]], axis=0)
        forward_value_list = jnp.concatenate([cached_v, new_kv[0, 1]], axis=0)
        backward_key_list = jnp.concatenate([cached_k, new_kv[1, 0]], axis=0)
        backward_value_list = jnp.concatenate([cached_v, new_kv[1, 1]], axis=0)
        attended = attend(
            forward_slice.reshape(seg_len, local_heads, head_size),
            forward_key_list,
            forward_value_list,
            segment_index[0, stretch, 0],
            cache_len,
        )[2]
        grad_query, grad_key, grad_value = attend_back(
            backward_slice.reshape(seg_len, local_heads, head_size),
            backward_key_list,
            backward_value_list,
            segment_index[0, stretch, 1],
            cache_len,
            grad_slice.reshape(seg_len, local_heads, head_size),
        )
        run_sums = jnp.stack([grad_key, grad_value])
        other_run = swapped_pairs(run_sums, "ctx")
        head_grads = (run_sums.astype(jnp.float32) + other_run.astype(jnp.float32)).astype(
            jnp.bfloat16
        )
        every_head = gather_heads(head_grads, rank_id, ctx_size)
        key_rows_heads = key_rows.reshape(local_width, kv_count, head_size)
        value_rows_heads = value_rows.reshape(local_width, kv_count, head_size)
        back_rows = jnp.einsum(
            "jtd,fjd->tf", every_head[:, 0], key_rows_heads, preferred_element_type=jnp.float32
        )
        back_rows = back_rows + jnp.einsum(
            "jtd,fjd->tf",
            every_head[:, 1],
            value_rows_heads,
            preferred_element_type=jnp.float32,
        )
        grad_acts = (
            grad_query.reshape(seg_len, -1).astype(jnp.float32) + back_rows.reshape(seg_len, -1)
        ).astype(jnp.bfloat16)
        returned = lax.all_to_all(
            jnp.stack([attended.reshape(ctx_size, local_rows, -1), grad_acts.reshape(ctx_size, local_rows, -1)]),
            "ctx",
            split_axis=1,
            concat_axis=3,
            tiled=True,
        )
        attn_rows = returned[0].reshape(local_rows, model_width)
        section_out = (forward_rows.astype(jnp.float32) + attn_rows.astype(jnp.float32)).astype(
            jnp.bfloat16
        )
        section_grad = input_grad(
            backward_rows, gain_row, returned[1].reshape(local_rows, model_width), grad_rows
        )
        forward_outs.append(passed_along(section_out, "pipe", 1))
        backward_outs.append(passed_along(section_grad, "pipe", -1))
    pipe_rank = lax.axis_index("pipe")
    arrived = jnp.stack(forward_outs)
    next_forward = jnp.where(pipe_rank == 0, jnp.roll(arrived, 1, axis=0), arrived)
    came_back = jnp.stack(backward_outs)
    next_backward = jnp.where(
        pipe_rank == lax.axis_size("pipe") - 1, jnp.roll(came_back, -1, axis=0), came_back
    )
    return (next_forward[None], next_backward[None])


def solution(mesh):
    in_specs = (
        P("pipe", None, "ctx", None),
        P("pipe", None, "ctx", None),
        P("pipe", None, "ctx", None),
        P("pipe", None, "ctx", None, None),
        P("pipe", None, "ctx", None, None),
        P("pipe", None, None),
        P("pipe", None, "ctx", None),
        P("pipe", None, "ctx", None),
        P("pipe", None, None),
    )
    out_specs = (P("pipe", None, "ctx", None), P("pipe", None, "ctx", None))
    return jax.shard_map(
        on_device, mesh=mesh, in_specs=in_specs, out_specs=out_specs, check_vma=False
    )
```

```python
import jax
import jax.numpy as jnp
from jax import lax
from jax.sharding import PartitionSpec as P

NEGATIVE = -1e30


def passed_along(array, axis, by):
    count = lax.axis_size(axis)
    return lax.ppermute(array, axis, [(i, (i + by) % count) for i in range(count)])


def swapped_pairs(array, axis):
    count = lax.axis_size(axis)
    return lax.ppermute(array, axis, [(i, i ^ 1) for i in range(count)])


def swapped_with(array, axis, mask):
    count = lax.axis_size(axis)
    return lax.ppermute(array, axis, [(i, i ^ mask) for i in range(count)])


def reduce_to_head(partial, rank_id, ctx_size, orders):
    rows = partial.shape[1]
    core = rank_id % 2
    half = rows // 2
    kept = lax.dynamic_slice_in_dim(partial, core * half, half, 1)
    given = lax.dynamic_slice_in_dim(partial, (1 - core) * half, half, 1)
    total = kept.astype(jnp.float32) + swapped_with(given, "ctx", 1).astype(jnp.float32)
    group = half // len(orders)
    finished = []
    for index, order in enumerate(orders):
        part = total[:, index * group : (index + 1) * group]
        for mask in order:
            bit = (rank_id // mask) % 2
            width = part.shape[2] // 2
            kept = lax.dynamic_slice_in_dim(part, bit * width, width, 2)
            given = lax.dynamic_slice_in_dim(part, (1 - bit) * width, width, 2)
            part = kept + swapped_with(given.astype(jnp.bfloat16), "ctx", mask).astype(jnp.float32)
        finished.append(part)
    mine = jnp.concatenate(finished, axis=1).astype(jnp.bfloat16)
    theirs = swapped_with(mine, "ctx", 1)
    return jnp.where(
        core == 0,
        jnp.concatenate([mine, theirs], axis=1),
        jnp.concatenate([theirs, mine], axis=1),
    )


def gather_heads(head_grads, rank_id, ctx_size):
    core = rank_id % 2
    rows = head_grads.shape[1]
    half = rows // 2
    held = lax.dynamic_slice_in_dim(head_grads, core * half, half, 1)[None]
    mask = 2
    while mask < ctx_size:
        other = swapped_with(held, "ctx", mask)
        bit = (rank_id // mask) % 2
        held = jnp.where(
            bit == 0,
            jnp.concatenate([held, other], axis=0),
            jnp.concatenate([other, held], axis=0),
        )
        mask *= 2
    other = swapped_with(held, "ctx", 1)
    return jnp.where(
        core == 0,
        jnp.concatenate([held, other], axis=2),
        jnp.concatenate([other, held], axis=2),
    )


def column_order(weight, order, head_size):
    natural = sorted(order, reverse=True)
    blocks = []
    for new_index in range(2 ** len(order)):
        old_index = 0
        for place, mask in enumerate(order):
            bit = (new_index >> (len(order) - 1 - place)) & 1
            old_index += bit << (len(order) - 1 - natural.index(mask))
        blocks.append(weight[..., old_index * head_size : (old_index + 1) * head_size])
    return jnp.concatenate(blocks, axis=-1)


def normalize(in_rows, gain_row):
    as_float = in_rows.astype(jnp.float32)
    inverse = lax.rsqrt(jnp.mean(as_float * as_float, axis=-1, keepdims=True) + 1e-05)
    normed = as_float * inverse
    return (normed, inverse, (normed * gain_row).astype(jnp.bfloat16))


def probabilities(queries, key_list, position, cache_len):
    seg_len = queries.shape[0]
    factor = queries.shape[-1] ** (-0.5)
    scores = (
        jnp.einsum("tgd,sd->gts", queries, key_list, preferred_element_type=jnp.float32) * factor
    )
    column = lax.broadcasted_iota(jnp.int32, (seg_len, key_list.shape[0]), 1)
    row_ids = lax.broadcasted_iota(jnp.int32, (seg_len, key_list.shape[0]), 0)
    visible = jnp.where(
        column < cache_len, column < position * seg_len, column - cache_len <= row_ids
    )
    scores = jnp.where(visible, scores, NEGATIVE)
    row_max = jnp.max(scores, axis=-1, keepdims=True)
    lifted = jnp.exp(scores - row_max)
    return lifted / jnp.sum(lifted, axis=-1, keepdims=True)


def attend(queries, key_list, value_list, position, cache_len):
    prob_full = probabilities(queries, key_list, position, cache_len)
    prob_half = prob_full.astype(jnp.bfloat16)
    attended = jnp.einsum(
        "gts,sd->tgd", prob_half, value_list, preferred_element_type=jnp.float32
    )
    return (prob_full, prob_half, attended.astype(jnp.bfloat16))


def attend_back(queries, key_list, value_list, position, cache_len, grad_heads):
    prob_full, prob_half, attended = attend(queries, key_list, value_list, position, cache_len)
    grad_prob = jnp.einsum(
        "tgd,sd->gts", grad_heads, value_list, preferred_element_type=jnp.float32
    )
    row_delta = jnp.sum(grad_heads.astype(jnp.float32) * attended.astype(jnp.float32), axis=-1)
    row_delta = jnp.transpose(row_delta, (1, 0))[..., None]
    factor = queries.shape[-1] ** (-0.5)
    grad_score = (prob_full * (grad_prob - row_delta) * factor).astype(jnp.bfloat16)
    grad_query = jnp.einsum(
        "gts,sd->tgd", grad_score, key_list, preferred_element_type=jnp.float32
    ).astype(jnp.bfloat16)
    grad_key = jnp.einsum(
        "gts,tgd->sd", grad_score[..., cache_len:], queries, preferred_element_type=jnp.float32
    )
    grad_value = jnp.einsum(
        "gts,tgd->sd", prob_half[..., cache_len:], grad_heads, preferred_element_type=jnp.float32
    )
    return (grad_query, grad_key.astype(jnp.bfloat16), grad_value.astype(jnp.bfloat16))


def input_grad(in_rows, gain_row, grad_acts, grad_rows):
    parts = normalize(in_rows, gain_row)
    normed = parts[0]
    inverse = parts[1]
    grad_normed = grad_acts.astype(jnp.float32) * gain_row
    grad_input = inverse * (
        grad_normed - normed * jnp.mean(grad_normed * normed, axis=-1, keepdims=True)
    )
    return (grad_rows.astype(jnp.float32) + grad_input).astype(jnp.bfloat16)


def on_device(
    forward_in,
    backward_in,
    grad_out,
    cached_keys,
    cached_values,
    norm_gain,
    key_weight,
    value_weight,
    segment_index,
):
    ctx_size = lax.axis_size("ctx")
    rank_id = lax.axis_index("ctx")
    stretch_count = forward_in.shape[1]
    local_rows = forward_in.shape[2]
    model_width = forward_in.shape[3]
    kv_count = cached_keys.shape[3]
    head_size = cached_keys.shape[4]
    seg_len = local_rows * ctx_size
    cache_local = cached_keys.shape[2]
    cache_len = cache_local * ctx_size
    head_count = model_width // head_size
    group_size = head_count // kv_count
    local_heads = head_count // ctx_size
    local_width = model_width // ctx_size
    kv_width = kv_count * head_size
    piece = kv_width // ctx_size
    copies = ctx_size // kv_count
    masks = []
    mask = ctx_size // 2
    while mask > 1:
        masks.append(mask)
        mask //= 2
    orders = (tuple(masks), (masks[-1],) + tuple(masks[:-1]))

    def per_owner(cache):
        picked = jnp.repeat(cache[0], copies, axis=2)
        return jnp.transpose(picked, (1, 2, 0, 3)).reshape(cache_local, ctx_size, -1)

    cache_rows = jnp.concatenate([per_owner(cached_keys), per_owner(cached_values)], axis=-1)

    forward_outs = []
    backward_outs = []
    for stretch in range(stretch_count):
        gain_row = norm_gain[0, stretch]
        key_rows = key_weight[0, stretch]
        value_rows = value_weight[0, stretch]
        forward_rows = forward_in[0, stretch]
        backward_rows = backward_in[0, stretch]
        grad_rows = grad_out[0, stretch]
        forward_acts = normalize(forward_rows, gain_row)[2]
        backward_acts = normalize(backward_rows, gain_row)[2]
        outgoing = [
            forward_acts.reshape(local_rows, ctx_size, local_width),
            backward_acts.reshape(local_rows, ctx_size, local_width),
            grad_rows.reshape(local_rows, ctx_size, local_width),
        ]
        if stretch == 0:
            outgoing.append(cache_rows)
        sent = lax.all_to_all(
            jnp.stack(outgoing), "ctx", split_axis=2, concat_axis=1, tiled=True
        )
        if stretch == 0:
            cache_heads = sent[3].reshape(cache_len, 2, stretch_count, head_size)
        forward_slice = sent[0].reshape(seg_len, local_width)
        backward_slice = sent[1].reshape(seg_len, local_width)
        grad_slice = sent[2].reshape(seg_len, local_width)
        both_slices = jnp.stack([forward_slice, backward_slice])
        group_rows = both_slices.reshape(2, 2, len(orders), -1, local_width)
        partial_value = jnp.stack(
            [
                jnp.stack(
                    [
                        jnp.einsum(
                            "btf,fe->bte",
                            group_rows[:, :, index].reshape(2, -1, local_width),
                            column_order(rows_weight, order, head_size),
                            preferred_element_type=jnp.float32,
                        ).reshape(2, 2, -1, kv_width)
                        for index, order in enumerate(orders)
                    ],
                    axis=2,
                )
                for rows_weight in (key_rows, value_rows)
            ]
        ).astype(jnp.bfloat16).reshape(4, seg_len, kv_width)
        new_kv = reduce_to_head(partial_value, rank_id, ctx_size, orders).reshape(
            2, 2, seg_len, head_size
        )
        new_kv = jnp.stack([new_kv[:, 0], new_kv[:, 1]], axis=0)
        cached_k = cache_heads[:, 0, stretch]
        cached_v = cache_heads[:, 1, stretch]
        forward_key_list = jnp.concatenate([cached_k, new_kv[0, 0]], axis=0)
        forward_value_list = jnp.concatenate([cached_v, new_kv[0, 1]], axis=0)
        backward_key_list = jnp.concatenate([cached_k, new_kv[1, 0]], axis=0)
        backward_value_list = jnp.concatenate([cached_v, new_kv[1, 1]], axis=0)
        if stretch > 0:
            (forward_slice, backward_slice, grad_slice, new_kv), _ = lax.optimization_barrier(
                ((forward_slice, backward_slice, grad_slice, new_kv), previous_outs)
            )
        attended = attend(
            forward_slice.reshape(seg_len, local_heads, head_size),
            forward_key_list,
            forward_value_list,
            segment_index[0, stretch, 0],
            cache_len,
        )[2]
        grad_query, grad_key, grad_value = attend_back(
            backward_slice.reshape(seg_len, local_heads, head_size),
            backward_key_list,
            backward_value_list,
            segment_index[0, stretch, 1],
            cache_len,
            grad_slice.reshape(seg_len, local_heads, head_size),
        )
        run_sums = jnp.stack([grad_key, grad_value])
        other_run = swapped_pairs(run_sums, "ctx")
        head_grads = (run_sums.astype(jnp.float32) + other_run.astype(jnp.float32)).astype(
            jnp.bfloat16
        )
        every_head = gather_heads(head_grads, rank_id, ctx_size)
        key_rows_heads = key_rows.reshape(local_width, kv_count, head_size)
        value_rows_heads = value_rows.reshape(local_width, kv_count, head_size)
        back_rows = jnp.einsum(
            "jtd,fjd->tf", every_head[:, 0], key_rows_heads, preferred_element_type=jnp.float32
        )
        back_rows = back_rows + jnp.einsum(
            "jtd,fjd->tf",
            every_head[:, 1],
            value_rows_heads,
            preferred_element_type=jnp.float32,
        )
        grad_acts = (
            grad_query.reshape(seg_len, -1).astype(jnp.float32) + back_rows.reshape(seg_len, -1)
        ).astype(jnp.bfloat16)
        returned = lax.all_to_all(
            jnp.stack([attended.reshape(ctx_size, local_rows, -1), grad_acts.reshape(ctx_size, local_rows, -1)]),
            "ctx",
            split_axis=1,
            concat_axis=3,
            tiled=True,
        )
        attn_rows = returned[0].reshape(local_rows, model_width)
        section_out = (forward_rows.astype(jnp.float32) + attn_rows.astype(jnp.float32)).astype(
            jnp.bfloat16
        )
        section_grad = input_grad(
            backward_rows, gain_row, returned[1].reshape(local_rows, model_width), grad_rows
        )
        previous_outs = (section_out, section_grad)
        forward_outs.append(passed_along(section_out, "pipe", 1))
        backward_outs.append(passed_along(section_grad, "pipe", -1))
    pipe_rank = lax.axis_index("pipe")
    arrived = jnp.stack(forward_outs)
    next_forward = jnp.where(pipe_rank == 0, jnp.roll(arrived, 1, axis=0), arrived)
    came_back = jnp.stack(backward_outs)
    next_backward = jnp.where(
        pipe_rank == lax.axis_size("pipe") - 1, jnp.roll(came_back, -1, axis=0), came_back
    )
    return (next_forward[None], next_backward[None])


def solution(mesh):
    in_specs = (
        P("pipe", None, "ctx", None),
        P("pipe", None, "ctx", None),
        P("pipe", None, "ctx", None),
        P("pipe", None, "ctx", None, None),
        P("pipe", None, "ctx", None, None),
        P("pipe", None, None),
        P("pipe", None, "ctx", None),
        P("pipe", None, "ctx", None),
        P("pipe", None, None),
    )
    out_specs = (P("pipe", None, "ctx", None), P("pipe", None, "ctx", None))
    return jax.shard_map(
        on_device, mesh=mesh, in_specs=in_specs, out_specs=out_specs, check_vma=False
    )
```

```python
import jax
import jax.numpy as jnp
from jax import lax
from jax.sharding import PartitionSpec as P

NEGATIVE = -1e30


def passed_along(array, axis, by):
    count = lax.axis_size(axis)
    return lax.ppermute(array, axis, [(i, (i + by) % count) for i in range(count)])


def swapped_pairs(array, axis):
    count = lax.axis_size(axis)
    return lax.ppermute(array, axis, [(i, i ^ 1) for i in range(count)])


def swapped_with(array, axis, mask):
    count = lax.axis_size(axis)
    return lax.ppermute(array, axis, [(i, i ^ mask) for i in range(count)])


def reduce_to_head(partial, rank_id, ctx_size, orders):
    rows = partial.shape[1]
    core = rank_id % 2
    half = rows // 2
    kept = lax.dynamic_slice_in_dim(partial, core * half, half, 1)
    given = lax.dynamic_slice_in_dim(partial, (1 - core) * half, half, 1)
    total = kept.astype(jnp.float32) + swapped_with(given, "ctx", 1).astype(jnp.float32)
    group = half // len(orders)
    finished = []
    for index, order in enumerate(orders):
        part = total[:, index * group : (index + 1) * group]
        for mask in order:
            bit = (rank_id // mask) % 2
            width = part.shape[2] // 2
            kept = lax.dynamic_slice_in_dim(part, bit * width, width, 2)
            given = lax.dynamic_slice_in_dim(part, (1 - bit) * width, width, 2)
            part = kept + swapped_with(given.astype(jnp.bfloat16), "ctx", mask).astype(jnp.float32)
        finished.append(part)
    mine = jnp.concatenate(finished, axis=1).astype(jnp.bfloat16)
    theirs = swapped_with(mine, "ctx", 1)
    return jnp.where(
        core == 0,
        jnp.concatenate([mine, theirs], axis=1),
        jnp.concatenate([theirs, mine], axis=1),
    )


def gather_heads(head_grads, rank_id, ctx_size):
    core = rank_id % 2
    rows = head_grads.shape[1]
    half = rows // 2
    held = lax.dynamic_slice_in_dim(head_grads, core * half, half, 1)[:, :, None]
    mask = 2
    while mask < ctx_size:
        other = swapped_with(held, "ctx", mask)
        bit = (rank_id // mask) % 2
        held = jnp.where(
            bit == 0,
            jnp.concatenate([held, other], axis=2),
            jnp.concatenate([other, held], axis=2),
        )
        mask *= 2
    other = swapped_with(held, "ctx", 1)
    every = jnp.where(
        core == 0,
        jnp.concatenate([held, other], axis=1),
        jnp.concatenate([other, held], axis=1),
    )
    return every.reshape(every.shape[0], rows, -1)


def column_order(weight, order, head_size):
    natural = sorted(order, reverse=True)
    blocks = []
    for new_index in range(2 ** len(order)):
        old_index = 0
        for place, mask in enumerate(order):
            bit = (new_index >> (len(order) - 1 - place)) & 1
            old_index += bit << (len(order) - 1 - natural.index(mask))
        blocks.append(weight[..., old_index * head_size : (old_index + 1) * head_size])
    return jnp.concatenate(blocks, axis=-1)


def normalize(in_rows, gain_row):
    as_float = in_rows.astype(jnp.float32)
    inverse = lax.rsqrt(jnp.mean(as_float * as_float, axis=-1, keepdims=True) + 1e-05)
    normed = as_float * inverse
    return (normed, inverse, (normed * gain_row).astype(jnp.bfloat16))


def probabilities(queries, key_list, position, cache_len):
    seg_len = queries.shape[0]
    factor = queries.shape[-1] ** (-0.5)
    scores = (
        jnp.einsum("tgd,sd->gts", queries, key_list, preferred_element_type=jnp.float32) * factor
    )
    column = lax.broadcasted_iota(jnp.int32, (seg_len, key_list.shape[0]), 1)
    row_ids = lax.broadcasted_iota(jnp.int32, (seg_len, key_list.shape[0]), 0)
    visible = jnp.where(
        column < cache_len, column < position * seg_len, column - cache_len <= row_ids
    )
    scores = jnp.where(visible, scores, NEGATIVE)
    row_max = jnp.max(scores, axis=-1, keepdims=True)
    lifted = jnp.exp(scores - row_max)
    return lifted / jnp.sum(lifted, axis=-1, keepdims=True)


def attend(queries, key_list, value_list, position, cache_len):
    prob_full = probabilities(queries, key_list, position, cache_len)
    prob_half = prob_full.astype(jnp.bfloat16)
    attended = jnp.einsum(
        "gts,sd->tgd", prob_half, value_list, preferred_element_type=jnp.float32
    )
    return (prob_full, prob_half, attended.astype(jnp.bfloat16))


def attend_back(queries, key_list, value_list, position, cache_len, grad_heads):
    prob_full, prob_half, attended = attend(queries, key_list, value_list, position, cache_len)
    grad_prob = jnp.einsum(
        "tgd,sd->gts", grad_heads, value_list, preferred_element_type=jnp.float32
    )
    row_delta = jnp.sum(grad_heads.astype(jnp.float32) * attended.astype(jnp.float32), axis=-1)
    row_delta = jnp.transpose(row_delta, (1, 0))[..., None]
    factor = queries.shape[-1] ** (-0.5)
    grad_score = (prob_full * (grad_prob - row_delta) * factor).astype(jnp.bfloat16)
    grad_query = jnp.einsum(
        "gts,sd->tgd", grad_score, key_list, preferred_element_type=jnp.float32
    ).astype(jnp.bfloat16)
    grad_key = jnp.einsum(
        "gts,tgd->sd", grad_score[..., cache_len:], queries, preferred_element_type=jnp.float32
    )
    grad_value = jnp.einsum(
        "gts,tgd->sd", prob_half[..., cache_len:], grad_heads, preferred_element_type=jnp.float32
    )
    return (grad_query, grad_key.astype(jnp.bfloat16), grad_value.astype(jnp.bfloat16))


def input_grad(in_rows, gain_row, grad_acts, grad_rows):
    parts = normalize(in_rows, gain_row)
    normed = parts[0]
    inverse = parts[1]
    grad_normed = grad_acts.astype(jnp.float32) * gain_row
    grad_input = inverse * (
        grad_normed - normed * jnp.mean(grad_normed * normed, axis=-1, keepdims=True)
    )
    return (grad_rows.astype(jnp.float32) + grad_input).astype(jnp.bfloat16)


def on_device(
    forward_in,
    backward_in,
    grad_out,
    cached_keys,
    cached_values,
    norm_gain,
    key_weight,
    value_weight,
    segment_index,
):
    ctx_size = lax.axis_size("ctx")
    rank_id = lax.axis_index("ctx")
    stretch_count = forward_in.shape[1]
    local_rows = forward_in.shape[2]
    model_width = forward_in.shape[3]
    kv_count = cached_keys.shape[3]
    head_size = cached_keys.shape[4]
    seg_len = local_rows * ctx_size
    cache_local = cached_keys.shape[2]
    cache_len = cache_local * ctx_size
    head_count = model_width // head_size
    group_size = head_count // kv_count
    local_heads = head_count // ctx_size
    local_width = model_width // ctx_size
    kv_width = kv_count * head_size
    piece = kv_width // ctx_size
    copies = ctx_size // kv_count
    masks = []
    mask = ctx_size // 2
    while mask > 1:
        masks.append(mask)
        mask //= 2
    orders = (tuple(masks), (masks[-1],) + tuple(masks[:-1]))

    def per_owner(cache):
        picked = jnp.repeat(cache[0], copies, axis=2)
        return jnp.transpose(picked, (1, 2, 0, 3)).reshape(cache_local, ctx_size, -1)

    cache_rows = jnp.concatenate([per_owner(cached_keys), per_owner(cached_values)], axis=-1)

    forward_outs = []
    backward_outs = []
    for stretch in range(stretch_count):
        gain_row = norm_gain[0, stretch]
        key_rows = key_weight[0, stretch]
        value_rows = value_weight[0, stretch]
        forward_rows = forward_in[0, stretch]
        backward_rows = backward_in[0, stretch]
        grad_rows = grad_out[0, stretch]
        forward_acts = normalize(forward_rows, gain_row)[2]
        backward_acts = normalize(backward_rows, gain_row)[2]
        outgoing = [
            forward_acts.reshape(local_rows, ctx_size, local_width),
            backward_acts.reshape(local_rows, ctx_size, local_width),
            grad_rows.reshape(local_rows, ctx_size, local_width),
        ]
        if stretch == 0:
            outgoing.append(cache_rows)
        sent = lax.all_to_all(
            jnp.stack(outgoing), "ctx", split_axis=2, concat_axis=1, tiled=True
        )
        if stretch == 0:
            cache_heads = sent[3].reshape(cache_len, 2, stretch_count, head_size)
        forward_slice = sent[0].reshape(seg_len, local_width)
        backward_slice = sent[1].reshape(seg_len, local_width)
        grad_slice = sent[2].reshape(seg_len, local_width)
        both_slices = jnp.stack([forward_slice, backward_slice])
        group_rows = both_slices.reshape(2, 2, len(orders), -1, local_width)
        partial_value = jnp.stack(
            [
                jnp.stack(
                    [
                        jnp.einsum(
                            "btf,fe->bte",
                            group_rows[:, :, index].reshape(2, -1, local_width),
                            column_order(rows_weight, order, head_size),
                            preferred_element_type=jnp.float32,
                        ).reshape(2, 2, -1, kv_width)
                        for index, order in enumerate(orders)
                    ],
                    axis=2,
                )
                for rows_weight in (key_rows, value_rows)
            ]
        ).astype(jnp.bfloat16).reshape(4, seg_len, kv_width)
        new_kv = reduce_to_head(partial_value, rank_id, ctx_size, orders).reshape(
            2, 2, seg_len, head_size
        )
        new_kv = jnp.stack([new_kv[:, 0], new_kv[:, 1]], axis=0)
        cached_k = cache_heads[:, 0, stretch]
        cached_v = cache_heads[:, 1, stretch]
        forward_key_list = jnp.concatenate([cached_k, new_kv[0, 0]], axis=0)
        forward_value_list = jnp.concatenate([cached_v, new_kv[0, 1]], axis=0)
        backward_key_list = jnp.concatenate([cached_k, new_kv[1, 0]], axis=0)
        backward_value_list = jnp.concatenate([cached_v, new_kv[1, 1]], axis=0)
        attended = attend(
            forward_slice.reshape(seg_len, local_heads, head_size),
            forward_key_list,
            forward_value_list,
            segment_index[0, stretch, 0],
            cache_len,
        )[2]
        grad_query, grad_key, grad_value = attend_back(
            backward_slice.reshape(seg_len, local_heads, head_size),
            backward_key_list,
            backward_value_list,
            segment_index[0, stretch, 1],
            cache_len,
            grad_slice.reshape(seg_len, local_heads, head_size),
        )
        run_sums = jnp.stack([grad_key, grad_value])
        other_run = swapped_pairs(run_sums, "ctx")
        head_grads = (run_sums.astype(jnp.float32) + other_run.astype(jnp.float32)).astype(
            jnp.bfloat16
        )
        every_head = gather_heads(head_grads, rank_id, ctx_size)
        back_rows = jnp.einsum(
            "te,fe->tf", every_head[0], key_rows, preferred_element_type=jnp.float32
        )
        back_rows = back_rows + jnp.einsum(
            "te,fe->tf", every_head[1], value_rows, preferred_element_type=jnp.float32
        )
        grad_acts = (
            grad_query.reshape(seg_len, -1).astype(jnp.float32) + back_rows.reshape(seg_len, -1)
        ).astype(jnp.bfloat16)
        returned = lax.all_to_all(
            jnp.stack([attended.reshape(ctx_size, local_rows, -1), grad_acts.reshape(ctx_size, local_rows, -1)]),
            "ctx",
            split_axis=1,
            concat_axis=3,
            tiled=True,
        )
        attn_rows = returned[0].reshape(local_rows, model_width)
        section_out = (forward_rows.astype(jnp.float32) + attn_rows.astype(jnp.float32)).astype(
            jnp.bfloat16
        )
        section_grad = input_grad(
            backward_rows, gain_row, returned[1].reshape(local_rows, model_width), grad_rows
        )
        forward_outs.append(passed_along(section_out, "pipe", 1))
        backward_outs.append(passed_along(section_grad, "pipe", -1))
    pipe_rank = lax.axis_index("pipe")
    arrived = jnp.stack(forward_outs)
    next_forward = jnp.where(pipe_rank == 0, jnp.roll(arrived, 1, axis=0), arrived)
    came_back = jnp.stack(backward_outs)
    next_backward = jnp.where(
        pipe_rank == lax.axis_size("pipe") - 1, jnp.roll(came_back, -1, axis=0), came_back
    )
    return (next_forward[None], next_backward[None])


def solution(mesh):
    in_specs = (
        P("pipe", None, "ctx", None),
        P("pipe", None, "ctx", None),
        P("pipe", None, "ctx", None),
        P("pipe", None, "ctx", None, None),
        P("pipe", None, "ctx", None, None),
        P("pipe", None, None),
        P("pipe", None, "ctx", None),
        P("pipe", None, "ctx", None),
        P("pipe", None, None),
    )
    out_specs = (P("pipe", None, "ctx", None), P("pipe", None, "ctx", None))
    return jax.shard_map(
        on_device, mesh=mesh, in_specs=in_specs, out_specs=out_specs, check_vma=False
    )
```

```python
import jax
import jax.numpy as jnp
from jax import lax
from jax.sharding import PartitionSpec as P

NEGATIVE = -1e30


def passed_along(array, axis, by):
    count = lax.axis_size(axis)
    return lax.ppermute(array, axis, [(i, (i + by) % count) for i in range(count)])


def swapped_pairs(array, axis):
    count = lax.axis_size(axis)
    return lax.ppermute(array, axis, [(i, i ^ 1) for i in range(count)])


def swapped_with(array, axis, mask):
    count = lax.axis_size(axis)
    return lax.ppermute(array, axis, [(i, i ^ mask) for i in range(count)])


def reduce_to_head(partial, rank_id, ctx_size, orders):
    rows = partial.shape[1]
    core = rank_id % 2
    half = rows // 2
    kept = lax.dynamic_slice_in_dim(partial, core * half, half, 1)
    given = lax.dynamic_slice_in_dim(partial, (1 - core) * half, half, 1)
    total = kept.astype(jnp.float32) + swapped_with(given, "ctx", 1).astype(jnp.float32)
    group = half // len(orders)
    finished = []
    for index, order in enumerate(orders):
        part = total[:, index * group : (index + 1) * group]
        for mask in order:
            bit = (rank_id // mask) % 2
            width = part.shape[2] // 2
            kept = lax.dynamic_slice_in_dim(part, bit * width, width, 2)
            given = lax.dynamic_slice_in_dim(part, (1 - bit) * width, width, 2)
            part = kept + swapped_with(given.astype(jnp.bfloat16), "ctx", mask).astype(jnp.float32)
        finished.append(part)
    mine = jnp.concatenate(finished, axis=1).astype(jnp.bfloat16)
    theirs = swapped_with(mine, "ctx", 1)
    return jnp.where(
        core == 0,
        jnp.concatenate([mine, theirs], axis=1),
        jnp.concatenate([theirs, mine], axis=1),
    )


def gather_heads(head_grads, rank_id, ctx_size):
    core = rank_id % 2
    rows = head_grads.shape[1]
    half = rows // 2
    held = lax.dynamic_slice_in_dim(head_grads, core * half, half, 1)[:, :, None]
    mask = 2
    while mask < ctx_size:
        other = swapped_with(held, "ctx", mask)
        bit = (rank_id // mask) % 2
        held = jnp.where(
            bit == 0,
            jnp.concatenate([held, other], axis=2),
            jnp.concatenate([other, held], axis=2),
        )
        mask *= 2
    other = swapped_with(held, "ctx", 1)
    every = jnp.where(
        core == 0,
        jnp.concatenate([held, other], axis=1),
        jnp.concatenate([other, held], axis=1),
    )
    return every.reshape(every.shape[0], rows, -1)


def column_order(weight, order, head_size):
    natural = sorted(order, reverse=True)
    blocks = []
    for new_index in range(2 ** len(order)):
        old_index = 0
        for place, mask in enumerate(order):
            bit = (new_index >> (len(order) - 1 - place)) & 1
            old_index += bit << (len(order) - 1 - natural.index(mask))
        blocks.append(weight[..., old_index * head_size : (old_index + 1) * head_size])
    return jnp.concatenate(blocks, axis=-1)


def normalize(in_rows, gain_row):
    as_float = in_rows.astype(jnp.float32)
    inverse = lax.rsqrt(jnp.mean(as_float * as_float, axis=-1, keepdims=True) + 1e-05)
    normed = as_float * inverse
    return (normed, inverse, (normed * gain_row).astype(jnp.bfloat16))


def probabilities(queries, key_list, position, cache_len):
    seg_len = queries.shape[0]
    factor = queries.shape[-1] ** (-0.5)
    scores = (
        jnp.einsum("tgd,sd->gts", queries, key_list, preferred_element_type=jnp.float32) * factor
    )
    column = lax.broadcasted_iota(jnp.int32, (seg_len, key_list.shape[0]), 1)
    row_ids = lax.broadcasted_iota(jnp.int32, (seg_len, key_list.shape[0]), 0)
    visible = jnp.where(
        column < cache_len, column < position * seg_len, column - cache_len <= row_ids
    )
    scores = jnp.where(visible, scores, NEGATIVE)
    row_max = jnp.max(scores, axis=-1, keepdims=True)
    lifted = jnp.exp(scores - row_max)
    return lifted / jnp.sum(lifted, axis=-1, keepdims=True)


def attend(queries, key_list, value_list, position, cache_len):
    prob_full = probabilities(queries, key_list, position, cache_len)
    prob_half = prob_full.astype(jnp.bfloat16)
    attended = jnp.einsum(
        "gts,sd->tgd", prob_half, value_list, preferred_element_type=jnp.float32
    )
    return (prob_full, prob_half, attended.astype(jnp.bfloat16))


def attend_back(queries, key_list, value_list, position, cache_len, grad_heads):
    prob_full, prob_half, attended = attend(queries, key_list, value_list, position, cache_len)
    grad_prob = jnp.einsum(
        "tgd,sd->gts", grad_heads, value_list, preferred_element_type=jnp.float32
    )
    row_delta = jnp.sum(grad_heads.astype(jnp.float32) * attended.astype(jnp.float32), axis=-1)
    row_delta = jnp.transpose(row_delta, (1, 0))[..., None]
    factor = queries.shape[-1] ** (-0.5)
    grad_score = (prob_full * (grad_prob - row_delta) * factor).astype(jnp.bfloat16)
    grad_query = jnp.einsum(
        "gts,sd->tgd", grad_score, key_list, preferred_element_type=jnp.float32
    ).astype(jnp.bfloat16)
    grad_key = jnp.einsum(
        "gts,tgd->sd", grad_score[..., cache_len:], queries, preferred_element_type=jnp.float32
    )
    grad_value = jnp.einsum(
        "gts,tgd->sd", prob_half[..., cache_len:], grad_heads, preferred_element_type=jnp.float32
    )
    return (grad_query, grad_key.astype(jnp.bfloat16), grad_value.astype(jnp.bfloat16))


def input_grad(in_rows, gain_row, grad_acts, grad_rows):
    parts = normalize(in_rows, gain_row)
    normed = parts[0]
    inverse = parts[1]
    grad_normed = grad_acts.astype(jnp.float32) * gain_row
    grad_input = inverse * (
        grad_normed - normed * jnp.mean(grad_normed * normed, axis=-1, keepdims=True)
    )
    return (grad_rows.astype(jnp.float32) + grad_input).astype(jnp.bfloat16)


def on_device(
    forward_in,
    backward_in,
    grad_out,
    cached_keys,
    cached_values,
    norm_gain,
    key_weight,
    value_weight,
    segment_index,
):
    ctx_size = lax.axis_size("ctx")
    rank_id = lax.axis_index("ctx")
    stretch_count = forward_in.shape[1]
    local_rows = forward_in.shape[2]
    model_width = forward_in.shape[3]
    kv_count = cached_keys.shape[3]
    head_size = cached_keys.shape[4]
    seg_len = local_rows * ctx_size
    cache_local = cached_keys.shape[2]
    cache_len = cache_local * ctx_size
    head_count = model_width // head_size
    group_size = head_count // kv_count
    local_heads = head_count // ctx_size
    local_width = model_width // ctx_size
    kv_width = kv_count * head_size
    piece = kv_width // ctx_size
    copies = ctx_size // kv_count
    masks = []
    mask = ctx_size // 2
    while mask > 1:
        masks.append(mask)
        mask //= 2
    orders = (tuple(masks), (masks[-1],) + tuple(masks[:-1]))

    def per_owner(cache):
        picked = jnp.repeat(cache[0], copies, axis=2)
        return jnp.transpose(picked, (1, 2, 0, 3)).reshape(cache_local, ctx_size, -1)

    cache_rows = jnp.concatenate([per_owner(cached_keys), per_owner(cached_values)], axis=-1)

    forward_outs = []
    backward_outs = []
    going_back = []
    for stretch in range(stretch_count):
        gain_row = norm_gain[0, stretch]
        key_rows = key_weight[0, stretch]
        value_rows = value_weight[0, stretch]
        forward_rows = forward_in[0, stretch]
        backward_rows = backward_in[0, stretch]
        grad_rows = grad_out[0, stretch]
        forward_acts = normalize(forward_rows, gain_row)[2]
        backward_acts = normalize(backward_rows, gain_row)[2]
        outgoing = [
            forward_acts.reshape(local_rows, ctx_size, local_width),
            backward_acts.reshape(local_rows, ctx_size, local_width),
            grad_rows.reshape(local_rows, ctx_size, local_width),
        ]
        if stretch == 0:
            outgoing.append(cache_rows)
        sent = lax.all_to_all(
            jnp.stack(outgoing), "ctx", split_axis=2, concat_axis=1, tiled=True
        )
        if stretch == 0:
            cache_heads = sent[3].reshape(cache_len, 2, stretch_count, head_size)
        forward_slice = sent[0].reshape(seg_len, local_width)
        backward_slice = sent[1].reshape(seg_len, local_width)
        grad_slice = sent[2].reshape(seg_len, local_width)
        both_slices = jnp.stack([forward_slice, backward_slice])
        group_rows = both_slices.reshape(2, 2, len(orders), -1, local_width)
        partial_value = jnp.stack(
            [
                jnp.stack(
                    [
                        jnp.einsum(
                            "btf,fe->bte",
                            group_rows[:, :, index].reshape(2, -1, local_width),
                            column_order(rows_weight, order, head_size),
                            preferred_element_type=jnp.float32,
                        ).reshape(2, 2, -1, kv_width)
                        for index, order in enumerate(orders)
                    ],
                    axis=2,
                )
                for rows_weight in (key_rows, value_rows)
            ]
        ).astype(jnp.bfloat16).reshape(4, seg_len, kv_width)
        new_kv = reduce_to_head(partial_value, rank_id, ctx_size, orders).reshape(
            2, 2, seg_len, head_size
        )
        new_kv = jnp.stack([new_kv[:, 0], new_kv[:, 1]], axis=0)
        cached_k = cache_heads[:, 0, stretch]
        cached_v = cache_heads[:, 1, stretch]
        forward_key_list = jnp.concatenate([cached_k, new_kv[0, 0]], axis=0)
        forward_value_list = jnp.concatenate([cached_v, new_kv[0, 1]], axis=0)
        backward_key_list = jnp.concatenate([cached_k, new_kv[1, 0]], axis=0)
        backward_value_list = jnp.concatenate([cached_v, new_kv[1, 1]], axis=0)
        attended = attend(
            forward_slice.reshape(seg_len, local_heads, head_size),
            forward_key_list,
            forward_value_list,
            segment_index[0, stretch, 0],
            cache_len,
        )[2]
        grad_query, grad_key, grad_value = attend_back(
            backward_slice.reshape(seg_len, local_heads, head_size),
            backward_key_list,
            backward_value_list,
            segment_index[0, stretch, 1],
            cache_len,
            grad_slice.reshape(seg_len, local_heads, head_size),
        )
        run_sums = jnp.stack([grad_key, grad_value])
        other_run = swapped_pairs(run_sums, "ctx")
        head_grads = (run_sums.astype(jnp.float32) + other_run.astype(jnp.float32)).astype(
            jnp.bfloat16
        )
        every_head = gather_heads(head_grads, rank_id, ctx_size)
        back_rows = jnp.einsum(
            "te,fe->tf", every_head[0], key_rows, preferred_element_type=jnp.float32
        )
        back_rows = back_rows + jnp.einsum(
            "te,fe->tf", every_head[1], value_rows, preferred_element_type=jnp.float32
        )
        grad_acts = (
            grad_query.reshape(seg_len, -1).astype(jnp.float32) + back_rows.reshape(seg_len, -1)
        ).astype(jnp.bfloat16)
        going_back.append(attended.reshape(ctx_size, local_rows, -1))
        going_back.append(grad_acts.reshape(ctx_size, local_rows, -1))
    returned = lax.all_to_all(
        jnp.stack(going_back), "ctx", split_axis=1, concat_axis=3, tiled=True
    )
    for stretch in range(stretch_count):
        gain_row = norm_gain[0, stretch]
        forward_rows = forward_in[0, stretch]
        backward_rows = backward_in[0, stretch]
        grad_rows = grad_out[0, stretch]
        attn_rows = returned[2 * stretch].reshape(local_rows, model_width)
        section_out = (forward_rows.astype(jnp.float32) + attn_rows.astype(jnp.float32)).astype(
            jnp.bfloat16
        )
        section_grad = input_grad(
            backward_rows,
            gain_row,
            returned[2 * stretch + 1].reshape(local_rows, model_width),
            grad_rows,
        )
        forward_outs.append(passed_along(section_out, "pipe", 1))
        backward_outs.append(passed_along(section_grad, "pipe", -1))
    pipe_rank = lax.axis_index("pipe")
    arrived = jnp.stack(forward_outs)
    next_forward = jnp.where(pipe_rank == 0, jnp.roll(arrived, 1, axis=0), arrived)
    came_back = jnp.stack(backward_outs)
    next_backward = jnp.where(
        pipe_rank == lax.axis_size("pipe") - 1, jnp.roll(came_back, -1, axis=0), came_back
    )
    return (next_forward[None], next_backward[None])


def solution(mesh):
    in_specs = (
        P("pipe", None, "ctx", None),
        P("pipe", None, "ctx", None),
        P("pipe", None, "ctx", None),
        P("pipe", None, "ctx", None, None),
        P("pipe", None, "ctx", None, None),
        P("pipe", None, None),
        P("pipe", None, "ctx", None),
        P("pipe", None, "ctx", None),
        P("pipe", None, None),
    )
    out_specs = (P("pipe", None, "ctx", None), P("pipe", None, "ctx", None))
    return jax.shard_map(
        on_device, mesh=mesh, in_specs=in_specs, out_specs=out_specs, check_vma=False
    )
```

```python
import jax
import jax.numpy as jnp
from jax import lax
from jax.sharding import PartitionSpec as P

NEGATIVE = -1e30


def passed_along(array, axis, by):
    count = lax.axis_size(axis)
    return lax.ppermute(array, axis, [(i, (i + by) % count) for i in range(count)])


def swapped_pairs(array, axis):
    count = lax.axis_size(axis)
    return lax.ppermute(array, axis, [(i, i ^ 1) for i in range(count)])


def swapped_with(array, axis, mask):
    count = lax.axis_size(axis)
    return lax.ppermute(array, axis, [(i, i ^ mask) for i in range(count)])


def reduce_to_head(partial, rank_id, ctx_size, orders):
    rows = partial.shape[1]
    core = rank_id % 2
    half = rows // 2
    kept = lax.dynamic_slice_in_dim(partial, core * half, half, 1)
    given = lax.dynamic_slice_in_dim(partial, (1 - core) * half, half, 1)
    total = kept.astype(jnp.float32) + swapped_with(given, "ctx", 1).astype(jnp.float32)
    group = half // len(orders)
    finished = []
    for index, order in enumerate(orders):
        part = total[:, index * group : (index + 1) * group]
        for mask in order:
            bit = (rank_id // mask) % 2
            width = part.shape[2] // 2
            kept = lax.dynamic_slice_in_dim(part, bit * width, width, 2)
            given = lax.dynamic_slice_in_dim(part, (1 - bit) * width, width, 2)
            part = kept + swapped_with(given.astype(jnp.bfloat16), "ctx", mask).astype(jnp.float32)
        finished.append(part)
    mine = jnp.concatenate(finished, axis=1).astype(jnp.bfloat16)
    theirs = swapped_with(mine, "ctx", 1)
    return jnp.where(
        core == 0,
        jnp.concatenate([mine, theirs], axis=1),
        jnp.concatenate([theirs, mine], axis=1),
    )


def gather_heads(head_grads, rank_id, ctx_size):
    core = rank_id % 2
    rows = head_grads.shape[1]
    half = rows // 2
    held = lax.dynamic_slice_in_dim(head_grads, core * half, half, 1)[:, :, None]
    mask = 2
    while mask < ctx_size:
        other = swapped_with(held, "ctx", mask)
        bit = (rank_id // mask) % 2
        held = jnp.where(
            bit == 0,
            jnp.concatenate([held, other], axis=2),
            jnp.concatenate([other, held], axis=2),
        )
        mask *= 2
    other = swapped_with(held, "ctx", 1)
    every = jnp.where(
        core == 0,
        jnp.concatenate([held, other], axis=1),
        jnp.concatenate([other, held], axis=1),
    )
    return every.reshape(every.shape[0], rows, -1)


def column_order(weight, order, head_size):
    natural = sorted(order, reverse=True)
    blocks = []
    for new_index in range(2 ** len(order)):
        old_index = 0
        for place, mask in enumerate(order):
            bit = (new_index >> (len(order) - 1 - place)) & 1
            old_index += bit << (len(order) - 1 - natural.index(mask))
        blocks.append(weight[..., old_index * head_size : (old_index + 1) * head_size])
    return jnp.concatenate(blocks, axis=-1)


def normalize(in_rows, gain_row):
    as_float = in_rows.astype(jnp.float32)
    inverse = lax.rsqrt(jnp.mean(as_float * as_float, axis=-1, keepdims=True) + 1e-05)
    normed = as_float * inverse
    return (normed, inverse, (normed * gain_row).astype(jnp.bfloat16))


def probabilities(queries, key_list, position, cache_len):
    seg_len = queries.shape[0]
    factor = queries.shape[-1] ** (-0.5)
    scores = (
        jnp.einsum("tgd,sd->gts", queries, key_list, preferred_element_type=jnp.float32) * factor
    )
    column = lax.broadcasted_iota(jnp.int32, (seg_len, key_list.shape[0]), 1)
    row_ids = lax.broadcasted_iota(jnp.int32, (seg_len, key_list.shape[0]), 0)
    visible = jnp.where(
        column < cache_len, column < position * seg_len, column - cache_len <= row_ids
    )
    scores = jnp.where(visible, scores, NEGATIVE)
    row_max = jnp.max(scores, axis=-1, keepdims=True)
    lifted = jnp.exp(scores - row_max)
    return lifted / jnp.sum(lifted, axis=-1, keepdims=True)


def attend(queries, key_list, value_list, position, cache_len):
    prob_full = probabilities(queries, key_list, position, cache_len)
    prob_half = prob_full.astype(jnp.bfloat16)
    attended = jnp.einsum(
        "gts,sd->tgd", prob_half, value_list, preferred_element_type=jnp.float32
    )
    return (prob_full, prob_half, attended.astype(jnp.bfloat16))


def attend_back(queries, key_list, value_list, position, cache_len, grad_heads):
    prob_full, prob_half, attended = attend(queries, key_list, value_list, position, cache_len)
    grad_prob = jnp.einsum(
        "tgd,sd->gts", grad_heads, value_list, preferred_element_type=jnp.float32
    )
    row_delta = jnp.sum(grad_heads.astype(jnp.float32) * attended.astype(jnp.float32), axis=-1)
    row_delta = jnp.transpose(row_delta, (1, 0))[..., None]
    factor = queries.shape[-1] ** (-0.5)
    grad_score = (prob_full * (grad_prob - row_delta) * factor).astype(jnp.bfloat16)
    grad_query = jnp.einsum(
        "gts,sd->tgd", grad_score, key_list, preferred_element_type=jnp.float32
    ).astype(jnp.bfloat16)
    grad_key = jnp.einsum(
        "gts,tgd->sd", grad_score[..., cache_len:], queries, preferred_element_type=jnp.float32
    )
    grad_value = jnp.einsum(
        "gts,tgd->sd", prob_half[..., cache_len:], grad_heads, preferred_element_type=jnp.float32
    )
    return (grad_query, grad_key.astype(jnp.bfloat16), grad_value.astype(jnp.bfloat16))


def input_grad(in_rows, gain_row, grad_acts, grad_rows):
    parts = normalize(in_rows, gain_row)
    normed = parts[0]
    inverse = parts[1]
    grad_normed = grad_acts.astype(jnp.float32) * gain_row
    grad_input = inverse * (
        grad_normed - normed * jnp.mean(grad_normed * normed, axis=-1, keepdims=True)
    )
    return (grad_rows.astype(jnp.float32) + grad_input).astype(jnp.bfloat16)


def on_device(
    forward_in,
    backward_in,
    grad_out,
    cached_keys,
    cached_values,
    norm_gain,
    key_weight,
    value_weight,
    segment_index,
):
    ctx_size = lax.axis_size("ctx")
    rank_id = lax.axis_index("ctx")
    stretch_count = forward_in.shape[1]
    local_rows = forward_in.shape[2]
    model_width = forward_in.shape[3]
    kv_count = cached_keys.shape[3]
    head_size = cached_keys.shape[4]
    seg_len = local_rows * ctx_size
    cache_local = cached_keys.shape[2]
    cache_len = cache_local * ctx_size
    head_count = model_width // head_size
    group_size = head_count // kv_count
    local_heads = head_count // ctx_size
    local_width = model_width // ctx_size
    kv_width = kv_count * head_size
    piece = kv_width // ctx_size
    copies = ctx_size // kv_count
    masks = []
    mask = ctx_size // 2
    while mask > 1:
        masks.append(mask)
        mask //= 2
    orders = (tuple(masks), (masks[-1],) + tuple(masks[:-1]))

    def per_owner(cache):
        picked = jnp.repeat(cache[0], copies, axis=2)
        return jnp.transpose(picked, (1, 2, 0, 3)).reshape(cache_local, ctx_size, -1)

    cache_rows = jnp.concatenate([per_owner(cached_keys), per_owner(cached_values)], axis=-1)

    forward_outs = []
    backward_outs = []
    for stretch in range(stretch_count):
        gain_row = norm_gain[0, stretch]
        key_rows = key_weight[0, stretch]
        value_rows = value_weight[0, stretch]
        forward_rows = forward_in[0, stretch]
        backward_rows = backward_in[0, stretch]
        grad_rows = grad_out[0, stretch]
        forward_acts = normalize(forward_rows, gain_row)[2]
        backward_acts = normalize(backward_rows, gain_row)[2]
        outgoing = [
            forward_acts.reshape(local_rows, ctx_size, local_width),
            backward_acts.reshape(local_rows, ctx_size, local_width),
            grad_rows.reshape(local_rows, ctx_size, local_width),
        ]
        if stretch == 0:
            outgoing.append(cache_rows)
        sent = lax.all_to_all(
            jnp.stack(outgoing), "ctx", split_axis=2, concat_axis=1, tiled=True
        )
        if stretch == 0:
            cache_heads = sent[3].reshape(cache_len, 2, stretch_count, head_size)
        forward_slice = sent[0].reshape(seg_len, local_width)
        backward_slice = sent[1].reshape(seg_len, local_width)
        grad_slice = sent[2].reshape(seg_len, local_width)
        both_slices = jnp.stack([forward_slice, backward_slice])
        group_rows = both_slices.reshape(2, 2, len(orders), -1, local_width)
        partial_value = jnp.stack(
            [
                jnp.stack(
                    [
                        jnp.einsum(
                            "btf,fe->bte",
                            group_rows[:, :, index].reshape(2, -1, local_width),
                            column_order(rows_weight, order, head_size),
                            preferred_element_type=jnp.float32,
                        ).reshape(2, 2, -1, kv_width)
                        for index, order in enumerate(orders)
                    ],
                    axis=2,
                )
                for rows_weight in (key_rows, value_rows)
            ]
        ).astype(jnp.bfloat16).reshape(4, seg_len, kv_width)
        new_kv = reduce_to_head(partial_value, rank_id, ctx_size, orders).reshape(
            2, 2, seg_len, head_size
        )
        new_kv = jnp.stack([new_kv[:, 0], new_kv[:, 1]], axis=0)
        cached_k = cache_heads[:, 0, stretch]
        cached_v = cache_heads[:, 1, stretch]
        forward_key_list = jnp.concatenate([cached_k, new_kv[0, 0]], axis=0)
        forward_value_list = jnp.concatenate([cached_v, new_kv[0, 1]], axis=0)
        backward_key_list = jnp.concatenate([cached_k, new_kv[1, 0]], axis=0)
        backward_value_list = jnp.concatenate([cached_v, new_kv[1, 1]], axis=0)
        attended = attend(
            forward_slice.reshape(seg_len, local_heads, head_size),
            forward_key_list,
            forward_value_list,
            segment_index[0, stretch, 0],
            cache_len,
        )[2]
        grad_query, grad_key, grad_value = attend_back(
            backward_slice.reshape(seg_len, local_heads, head_size),
            backward_key_list,
            backward_value_list,
            segment_index[0, stretch, 1],
            cache_len,
            grad_slice.reshape(seg_len, local_heads, head_size),
        )
        run_sums = jnp.stack([grad_key, grad_value])
        other_run = swapped_pairs(run_sums, "ctx")
        head_grads = (run_sums.astype(jnp.float32) + other_run.astype(jnp.float32)).astype(
            jnp.bfloat16
        )
        every_head = gather_heads(head_grads, rank_id, ctx_size)
        back_rows = jnp.einsum(
            "te,fe->tf", every_head[0], key_rows, preferred_element_type=jnp.float32
        )
        back_rows = back_rows + jnp.einsum(
            "te,fe->tf", every_head[1], value_rows, preferred_element_type=jnp.float32
        )
        grad_acts = (
            grad_query.reshape(seg_len, -1).astype(jnp.float32) + back_rows.reshape(seg_len, -1)
        ).astype(jnp.bfloat16)
        returned = lax.all_to_all(
            jnp.stack([attended.reshape(ctx_size, local_rows, -1), grad_acts.reshape(ctx_size, local_rows, -1)]),
            "ctx",
            split_axis=1,
            concat_axis=3,
            tiled=True,
        )
        attn_rows = returned[0].reshape(local_rows, model_width)
        section_out = (forward_rows.astype(jnp.float32) + attn_rows.astype(jnp.float32)).astype(
            jnp.bfloat16
        )
        section_grad = input_grad(
            backward_rows, gain_row, returned[1].reshape(local_rows, model_width), grad_rows
        )
        forward_outs.append(section_out)
        backward_outs.append(section_grad)
    pipe_rank = lax.axis_index("pipe")
    pipe_last = lax.axis_size("pipe") - 1
    forward_stack = jnp.stack(forward_outs)
    backward_stack = jnp.stack(backward_outs)
    next_forward = passed_along(
        jnp.where(pipe_rank == pipe_last, jnp.roll(forward_stack, 1, axis=0), forward_stack),
        "pipe",
        1,
    )
    next_backward = passed_along(
        jnp.where(pipe_rank == 0, jnp.roll(backward_stack, -1, axis=0), backward_stack),
        "pipe",
        -1,
    )
    return (next_forward[None], next_backward[None])


def solution(mesh):
    in_specs = (
        P("pipe", None, "ctx", None),
        P("pipe", None, "ctx", None),
        P("pipe", None, "ctx", None),
        P("pipe", None, "ctx", None, None),
        P("pipe", None, "ctx", None, None),
        P("pipe", None, None),
        P("pipe", None, "ctx", None),
        P("pipe", None, "ctx", None),
        P("pipe", None, None),
    )
    out_specs = (P("pipe", None, "ctx", None), P("pipe", None, "ctx", None))
    return jax.shard_map(
        on_device, mesh=mesh, in_specs=in_specs, out_specs=out_specs, check_vma=False
    )
```
